256 devices in a mesh: seq: 16 (over y, x_hi, core), dp: 16 (over x_lo, z).
Axes of the slice: x: 4 (x_hi: 2, x_lo: 2; x = x_hi * 2 + x_lo), y: 4, z: 8, core: 2. Of those that a mesh axis runs over, the one named last changes fastest.
Arguments:
- features: bfloat16 [32, 6144, 768], P('dp', 'seq'), may hold values from -32 to 32
- weight: bfloat16 [5, 768, 768], replicated, may hold values from -0.09375 to 0.09375
- cotangent: bfloat16 [32, 3072, 768], P('dp', 'seq'), may hold values from -6 to 6
Outputs:
- trunk_input: bfloat16 [32, 3072, 768], P('dp', None, 'seq')
- input_grad: bfloat16 [32, 6144, 768], P('dp', 'seq')
- weight_grad: float32 [5, 768, 768], P(None, 'dp', 'seq')
The draws below stay inside these ranges and needn't reach their ends.
All inputs are finite; a program needn't handle non-finite values.
Results may differ from the reference program's by a relative error of at most 0.0027.
Values may be sent and summed in bfloat16 or wider, within the bound.
No kernel may reach another device: no remote copies, remote signals or barrier semaphores. Data moves between devices by JAX's collectives and lax.ppermute only.
A program may use at most 128 MiB of HBM per device.

```python
import jax
import jax.numpy as jnp
from jax import lax

C = 768
W = 5
LEN = 6144
POOLED = 3072
BATCH = 32


def draw_features(key, part):
    first, second, third = jax.random.split(key, 3)
    shape = (BATCH, LEN, C)
    base = jax.random.truncated_normal(first, -3.5, 3.5, shape, jnp.float32)
    rows = jnp.exp(jax.random.uniform(second, (BATCH, LEN, 1), jnp.float32, jnp.log(0.3), jnp.log(3.0)))
    columns = jnp.exp(jax.random.uniform(third, (1, 1, C), jnp.float32, jnp.log(0.3), jnp.log(3.0)))
    return (base * rows * columns).astype(jnp.bfloat16)


def raised(drawn, stream_key, source, target, shards_of, factor):
    def block_of(axis_at):
        return (jnp.arange(drawn.shape[axis_at]) // (drawn.shape[axis_at] // shards_of)).reshape((-1,) + (1,) * (drawn.ndim - 1 - axis_at))

    near = jax.random.permutation(stream_key, shards_of)[block_of(target)]
    other_side = (block_of(target) + shards_of // 2) % shards_of
    return jnp.where((block_of(source) == near) | (block_of(source) == other_side), factor * drawn, drawn)


def level_of(stream_key, extent, pieces, least, high):
    def one(position, blocks):
        steps = jax.random.uniform(jax.random.fold_in(jax.random.fold_in(stream_key, 6), position), (blocks,), jnp.float32, least / len(pieces), high / len(pieces))
        return jnp.repeat(jnp.exp(steps), extent[position] // blocks).reshape((-1,) + (1,) * (len(extent) - position - 1))

    gain = one(*pieces[0])
    for cut in pieces[1:]:
        gain = gain * one(*cut)
    return gain


def scatter_about(key, shape, scale, limit, pieces=(), kind=jnp.bfloat16):
    factor_of = level_of(key, shape, pieces, -0.22, 0.18) if pieces else 1.0
    drawn = jax.random.normal(key, shape, jnp.float32) * scale * factor_of
    return jnp.minimum(jnp.maximum(drawn, -limit), limit).astype(kind)


def gaussian_with(stream_key, extent, deviation, most, cuts, heavy, held_as=jnp.bfloat16):
    drawn = deviation * jax.random.normal(stream_key, extent, jnp.float32)
    if cuts:
        drawn = drawn * level_of(stream_key, extent, cuts, -0.22, 0.18)
    return jnp.clip(raised(drawn, jax.random.fold_in(stream_key, 3), *heavy), -most, most).astype(held_as)


def setup_inputs(seed: int = 0) -> dict:
    key_list = jax.random.split(jax.random.key(seed), 4)
    return {
        "features": draw_features(jax.random.fold_in(key_list[3], 71), 0),
        "weight": scatter_about(key_list[1], (W, C, C), (W * C) ** -0.5, 0.09375),
        "cotangent": gaussian_with(key_list[2], (BATCH, POOLED, C), 1.0, 6.0, ((0, 16), (1, 16)), (1, 2, 16, 2.0)),
    }


epsilon = 1e-06
root_half = 0.7071067811865476
inv_root_two_pi = 0.3989422804014327

def gaussian_unit(value):
    return 0.5 * value * (1.0 + jax.scipy.special.erf(value * root_half))

def gaussian_slope(value):
    return 0.5 * (1.0 + jax.scipy.special.erf(value * root_half)) + value * inv_root_two_pi * jnp.exp(-0.5 * value * value)

def one_sequence(pair, weight):
    features, cotangent = pair
    length = features.shape[0]
    taps = weight.shape[0]
    reach = taps // 2
    weights32 = weight.astype(jnp.float32)
    floats = features.astype(jnp.float32)
    inverse = lax.rsqrt(lax.optimization_barrier(jnp.mean(floats * floats, axis=-1, keepdims=True)) + epsilon)
    normed = floats * inverse
    activations = gaussian_unit(normed).astype(jnp.bfloat16)
    padded = jnp.pad(activations, ((reach, reach), (0, 0)))
    window = jnp.stack([padded[offset:offset + length] for offset in range(taps)], axis=1).astype(jnp.float32)
    mixed = jnp.einsum('lki,kio->lo', window, weights32)
    summed = floats + mixed
    pooled = (0.5 * (summed[0::2] + summed[1::2])).astype(jnp.bfloat16)
    upward = 0.5 * jnp.repeat(cotangent.astype(jnp.float32), 2, axis=0)
    branch_grad = upward.astype(jnp.bfloat16)
    padded_grad = jnp.pad(branch_grad, ((reach, reach), (0, 0)))
    grad_window = jnp.stack([padded_grad[offset:offset + length] for offset in range(taps)], axis=1).astype(jnp.float32)
    act_grad = jnp.einsum('lko,kio->li', grad_window, weights32[::-1])
    slope_grad = act_grad * gaussian_slope(normed)
    centred = lax.optimization_barrier(jnp.mean(slope_grad * floats, axis=-1, keepdims=True))
    input_grad = (upward + inverse * slope_grad - floats * inverse ** 3 * centred).astype(jnp.bfloat16)
    kernel_grad = jnp.einsum('lki,lo->kio', window, branch_grad.astype(jnp.float32))
    return (pooled, input_grad, kernel_grad)

def reference(features, weight, cotangent):
    pooled, input_grad, kernel_grad = lax.map(lambda pair: one_sequence(pair, weight), (features, cotangent))
    return (pooled, input_grad, lax.optimization_barrier(jnp.sum(kernel_grad, axis=0)))
```

```python
import jax
import jax.numpy as jnp
from jax import lax
from jax.sharding import PartitionSpec as P

epsilon = 1e-06
root_half = 0.7071067811865476
inv_root_two_pi = 0.3989422804014327


def with_halo(block, sides, width):
    for axis, dim in sides:
        count = lax.axis_size(axis)
        forward = [(i, i + 1) for i in range(count - 1)]
        backward = [(target, source) for source, target in forward]
        low = lax.ppermute(
            lax.slice_in_dim(block, block.shape[dim] - width, None, axis=dim), axis, forward
        )
        high = lax.ppermute(lax.slice_in_dim(block, 0, width, axis=dim), axis, backward)
        block = jnp.concatenate([low, block, high], axis=dim)
    return block


def halved(block, axis, bit, dim):
    count = lax.axis_size(axis)
    partners = [(i, i ^ (1 << bit)) for i in range(count)]
    mine = (lax.axis_index(axis) >> bit) & 1
    half = block.shape[dim] // 2
    keep = lax.dynamic_slice_in_dim(block, mine * half, half, axis=dim)
    send = lax.dynamic_slice_in_dim(block, (1 - mine) * half, half, axis=dim)
    return keep + lax.ppermute(send, axis, partners)


def reordered(block, bits, pieces, piece):
    lead = block.shape[:-1]
    width = block.shape[-1] // (16 * pieces)
    split = block.reshape(lead + (2, 2, 2, 2, pieces, width))
    split = lax.index_in_dim(split, piece, axis=len(lead) + 4, keepdims=False)
    base = len(lead)
    order = tuple(range(base)) + tuple(base + 3 - bit for bit in bits) + (base + 4,)
    return jnp.transpose(split, order).reshape(lead + (16 * width,))


CHAINS = (
    (("seq", 0), ("seq", 2), ("seq", 1), ("dp", 0), ("seq", 3), ("dp", 3), ("dp", 1), ("dp", 2)),
    (("seq", 0), ("seq", 1), ("dp", 0), ("seq", 2), ("seq", 3), ("dp", 3), ("dp", 1), ("dp", 2)),
    (("seq", 0), ("dp", 0), ("seq", 2), ("seq", 1), ("seq", 3), ("dp", 3), ("dp", 1), ("dp", 2)),
)


def gaussian_unit(value):
    return 0.5 * value * (1.0 + jax.scipy.special.erf(value * root_half))


def gaussian_slope(value):
    return 0.5 * (
        1.0 + jax.scipy.special.erf(value * root_half)
    ) + value * inv_root_two_pi * jnp.exp(-0.5 * value * value)


def windows(padded, length, taps):
    return jnp.stack([padded[:, offset : offset + length] for offset in range(taps)], axis=2)


def shards(features, weight, cotangent):
    taps = weight.shape[0]
    channels = weight.shape[2]
    batch = features.shape[0]
    length = features.shape[1]
    reach = taps // 2
    floats = features.astype(jnp.float32)
    inverse = lax.rsqrt(jnp.mean(floats * floats, axis=-1, keepdims=True) + epsilon)
    normed = floats * inverse
    activations = gaussian_unit(normed).astype(jnp.bfloat16)
    halves = 0.5 * cotangent.astype(jnp.float32)
    upward = jnp.broadcast_to(halves[:, :, None, :], (batch, length // 2, 2, channels)).reshape(
        batch, length, channels
    )
    branch_grad = upward.astype(jnp.bfloat16)
    padded_acts = with_halo(activations, (("seq", 1),), reach)
    padded_grad = with_halo(branch_grad, (("seq", 1),), reach)
    window = windows(padded_acts, length, taps)
    mixed = jnp.einsum("blki,kio->blo", window, weight, preferred_element_type=jnp.float32)
    summed = floats + mixed
    paired = summed.reshape(batch, length // 2, 2, channels)
    pooled = (0.5 * (paired[:, :, 0] + paired[:, :, 1])).astype(jnp.bfloat16)
    trunk_input = lax.all_to_all(pooled, "seq", split_axis=2, concat_axis=1, tiled=True)
    grad_window = windows(padded_grad, length, taps)
    act_grad = jnp.einsum(
        "blko,kio->bli", grad_window, weight[::-1], preferred_element_type=jnp.float32
    )
    slope_grad = act_grad * gaussian_slope(normed)
    centred = jnp.mean(slope_grad * floats, axis=-1, keepdims=True)
    input_grad = (upward + inverse * slope_grad - floats * inverse**3 * centred).astype(
        jnp.bfloat16
    )
    dp_order = tuple(bit for axis, bit in CHAINS[0] if axis == "dp")
    act_window = windows(reordered(padded_acts, dp_order, 1, 0), length, taps)
    shares = []
    for piece, steps in enumerate(CHAINS):
        seq_order = tuple(bit for axis, bit in steps if axis == "seq")
        partial = jnp.einsum(
            "blo,blki->oki",
            reordered(branch_grad, seq_order, len(CHAINS), piece),
            act_window,
            preferred_element_type=jnp.float32,
        )
        for axis, bit in steps:
            partial = halved(partial, axis, bit, 0 if axis == "seq" else 2)
        shares.append(partial)
    weight_grad = jnp.transpose(jnp.concatenate(shares, axis=0), (1, 2, 0))
    return (trunk_input, input_grad, weight_grad)


def solution(mesh):
    return jax.shard_map(
        shards,
        mesh=mesh,
        in_specs=(P("dp", "seq", None), P(), P("dp", "seq", None)),
        out_specs=(P("dp", None, "seq"), P("dp", "seq", None), P(None, "dp", "seq")),
        check_vma=False,
    )
```

```python
import jax
import jax.numpy as jnp
from jax import lax
from jax.sharding import PartitionSpec as P
import numpy as np

epsilon = 1e-06
root_half = 0.7071067811865476
inv_root_two_pi = 0.3989422804014327


def with_halo(block, sides, width):
    for axis, dim in sides:
        count = lax.axis_size(axis)
        forward = [(i, i + 1) for i in range(count - 1)]
        backward = [(target, source) for source, target in forward]
        low = lax.ppermute(
            lax.slice_in_dim(block, block.shape[dim] - width, None, axis=dim), axis, forward
        )
        high = lax.ppermute(lax.slice_in_dim(block, 0, width, axis=dim), axis, backward)
        block = jnp.concatenate([low, block, high], axis=dim)
    return block


def halved(block, axis, bit, dim):
    count = lax.axis_size(axis)
    partners = [(i, i ^ (1 << bit)) for i in range(count)]
    mine = (lax.axis_index(axis) >> bit) & 1
    half = block.shape[dim] // 2
    keep = lax.dynamic_slice_in_dim(block, mine * half, half, axis=dim)
    send = lax.dynamic_slice_in_dim(block, (1 - mine) * half, half, axis=dim)
    return keep + lax.ppermute(send, axis, partners)


def picked(block, bits, pieces, piece):
    width = block.shape[-1] // (16 * pieces)
    sources = []
    for place in range(16 * width):
        code, rest = divmod(place, width)
        index = 0
        for step, bit in enumerate(bits):
            index |= ((code >> (3 - step)) & 1) << bit
        sources.append((index * pieces + piece) * width + rest)
    rows = lax.broadcasted_iota(jnp.int32, (block.shape[-1], len(sources)), 0)
    one_hot = (rows == jnp.asarray(np.array(sources, np.int32))[None, :]).astype(block.dtype)
    moved = jnp.einsum("blc,co->blo", block, one_hot, preferred_element_type=jnp.float32)
    return moved.astype(block.dtype)


CHAINS = (
    (("seq", 0), ("seq", 2), ("seq", 1), ("dp", 0), ("seq", 3), ("dp", 3), ("dp", 1), ("dp", 2)),
    (("seq", 0), ("seq", 1), ("dp", 0), ("seq", 2), ("seq", 3), ("dp", 3), ("dp", 1), ("dp", 2)),
    (("seq", 0), ("dp", 0), ("seq", 2), ("seq", 1), ("seq", 3), ("dp", 3), ("dp", 1), ("dp", 2)),
)


def gaussian_unit(value):
    return 0.5 * value * (1.0 + jax.scipy.special.erf(value * root_half))


def gaussian_slope(value):
    return 0.5 * (
        1.0 + jax.scipy.special.erf(value * root_half)
    ) + value * inv_root_two_pi * jnp.exp(-0.5 * value * value)


def windows(padded, length, taps):
    return jnp.stack([padded[:, offset : offset + length] for offset in range(taps)], axis=2)


def shards(features, weight, cotangent):
    taps = weight.shape[0]
    channels = weight.shape[2]
    batch = features.shape[0]
    length = features.shape[1]
    reach = taps // 2
    floats = features.astype(jnp.float32)
    inverse = lax.rsqrt(jnp.mean(floats * floats, axis=-1, keepdims=True) + epsilon)
    normed = floats * inverse
    activations = gaussian_unit(normed).astype(jnp.bfloat16)
    halves = 0.5 * cotangent.astype(jnp.float32)
    upward = jnp.broadcast_to(halves[:, :, None, :], (batch, length // 2, 2, channels)).reshape(
        batch, length, channels
    )
    branch_grad = upward.astype(jnp.bfloat16)
    padded_acts = with_halo(activations, (("seq", 1),), reach)
    padded_grad = with_halo(branch_grad, (("seq", 1),), reach)
    window = windows(padded_acts, length, taps)
    mixed = jnp.einsum("blki,kio->blo", window, weight, preferred_element_type=jnp.float32)
    summed = floats + mixed
    paired = summed.reshape(batch, length // 2, 2, channels)
    pooled = (0.5 * (paired[:, :, 0] + paired[:, :, 1])).astype(jnp.bfloat16)
    trunk_input = lax.all_to_all(pooled, "seq", split_axis=2, concat_axis=1, tiled=True)
    grad_window = jnp.stack(
        [padded_grad[:, taps - 1 - k : taps - 1 - k + length] for k in range(taps)], axis=2
    )
    act_grad = jnp.einsum("blko,kio->bli", grad_window, weight, preferred_element_type=jnp.float32)
    slope_grad = act_grad * gaussian_slope(normed)
    centred = jnp.mean(slope_grad * floats, axis=-1, keepdims=True)
    input_grad = (upward + inverse * slope_grad - floats * inverse**3 * centred).astype(
        jnp.bfloat16
    )
    dp_order = tuple(bit for axis, bit in CHAINS[0] if axis == "dp")
    act_window = windows(picked(padded_acts, dp_order, 1, 0), length, taps)
    shares = []
    for piece, steps in enumerate(CHAINS):
        seq_order = tuple(bit for axis, bit in steps if axis == "seq")
        partial = jnp.einsum(
            "blo,blki->oki",
            picked(branch_grad, seq_order, len(CHAINS), piece),
            act_window,
            preferred_element_type=jnp.float32,
        )
        for axis, bit in steps:
            partial = halved(partial, axis, bit, 0 if axis == "seq" else 2)
        shares.append(partial)
    weight_grad = jnp.transpose(jnp.concatenate(shares, axis=0), (1, 2, 0))
    return (trunk_input, input_grad, weight_grad)


def solution(mesh):
    return jax.shard_map(
        shards,
        mesh=mesh,
        in_specs=(P("dp", "seq", None), P(), P("dp", "seq", None)),
        out_specs=(P("dp", None, "seq"), P("dp", "seq", None), P(None, "dp", "seq")),
        check_vma=False,
    )
```

```python
import jax
import jax.numpy as jnp
from jax import lax
from jax.sharding import PartitionSpec as P
import numpy as np

epsilon = 1e-06
root_half = 0.7071067811865476
inv_root_two_pi = 0.3989422804014327


def with_halo(block, sides, width):
    for axis, dim in sides:
        count = lax.axis_size(axis)
        forward = [(i, i + 1) for i in range(count - 1)]
        backward = [(target, source) for source, target in forward]
        low = lax.ppermute(
            lax.slice_in_dim(block, block.shape[dim] - width, None, axis=dim), axis, forward
        )
        high = lax.ppermute(lax.slice_in_dim(block, 0, width, axis=dim), axis, backward)
        block = jnp.concatenate([low, block, high], axis=dim)
    return block


def halved(block, axis, bit):
    count = lax.axis_size(axis)
    partners = [(i, i ^ (1 << bit)) for i in range(count)]
    mine = (lax.axis_index(axis) >> bit) & 1
    half = block.shape[0] // 2
    keep = lax.dynamic_slice_in_dim(block, mine * half, half, axis=0)
    send = lax.dynamic_slice_in_dim(block, (1 - mine) * half, half, axis=0)
    return keep + lax.ppermute(send, axis, partners)


def exchanged(block, axis):
    count = lax.axis_size(axis)
    rows, taps, width = block.shape
    parts = jnp.transpose(block.reshape(rows, taps, count, width // count), (2, 0, 1, 3))
    return jnp.sum(lax.all_to_all(parts, axis, 0, 0), axis=0)


def picked(block, orders):
    pieces = len(orders)
    width = block.shape[-1] // (16 * pieces)
    sources = []
    for piece, bits in enumerate(orders):
        for place in range(16 * width):
            code, rest = divmod(place, width)
            index = 0
            for step, bit in enumerate(bits):
                index |= ((code >> (len(bits) - 1 - step)) & 1) << bit
            sources.append((index * pieces + piece) * width + rest)
    rows = lax.broadcasted_iota(jnp.int32, (block.shape[-1], len(sources)), 0)
    one_hot = (rows == jnp.asarray(np.array(sources, np.int32))[None, :]).astype(block.dtype)
    moved = jnp.einsum("blc,co->blo", block, one_hot, preferred_element_type=jnp.float32)
    return moved.astype(block.dtype)


CHAINS = (
    (("seq", 0), ("seq", 2), ("seq", 1), ("seq", 3), ("dp", None)),
    (("seq", 0), ("seq", 1), ("seq", 2), ("seq", 3), ("dp", None)),
    (("seq", 0), ("dp", None), ("seq", 2), ("seq", 1), ("seq", 3)),
)


def gaussian_unit(value):
    return 0.5 * value * (1.0 + jax.scipy.special.erf(value * root_half))


def gaussian_slope(value):
    return 0.5 * (
        1.0 + jax.scipy.special.erf(value * root_half)
    ) + value * inv_root_two_pi * jnp.exp(-0.5 * value * value)


def windows(padded, length, taps):
    return jnp.stack([padded[:, offset : offset + length] for offset in range(taps)], axis=2)


def shards(features, weight, cotangent):
    taps = weight.shape[0]
    channels = weight.shape[2]
    batch = features.shape[0]
    length = features.shape[1]
    reach = taps // 2
    floats = features.astype(jnp.float32)
    inverse = lax.rsqrt(jnp.mean(floats * floats, axis=-1, keepdims=True) + epsilon)
    normed = floats * inverse
    activations = gaussian_unit(normed).astype(jnp.bfloat16)
    halves = 0.5 * cotangent.astype(jnp.float32)
    upward = jnp.broadcast_to(halves[:, :, None, :], (batch, length // 2, 2, channels)).reshape(
        batch, length, channels
    )
    branch_grad = upward.astype(jnp.bfloat16)
    padded_acts = with_halo(activations, (("seq", 1),), reach)
    padded_grad = with_halo(branch_grad, (("seq", 1),), reach)
    window = windows(padded_acts, length, taps)
    mixed = jnp.einsum("blki,kio->blo", window, weight, preferred_element_type=jnp.float32)
    summed = floats + mixed
    paired = summed.reshape(batch, length // 2, 2, channels)
    pooled = (0.5 * (paired[:, :, 0] + paired[:, :, 1])).astype(jnp.bfloat16)
    trunk_input = lax.all_to_all(pooled, "seq", split_axis=2, concat_axis=1, tiled=True)
    grad_window = jnp.stack(
        [padded_grad[:, taps - 1 - k : taps - 1 - k + length] for k in range(taps)], axis=2
    )
    act_grad = jnp.einsum("blko,kio->bli", grad_window, weight, preferred_element_type=jnp.float32)
    slope_grad = act_grad * gaussian_slope(normed)
    centred = jnp.mean(slope_grad * floats, axis=-1, keepdims=True)
    input_grad = (upward + inverse * slope_grad - floats * inverse**3 * centred).astype(
        jnp.bfloat16
    )
    orders = [tuple(bit for axis, bit in steps if axis == "seq") for steps in CHAINS]
    partial = jnp.einsum(
        "blo,blki->oki", picked(branch_grad, orders), window, preferred_element_type=jnp.float32
    )
    share = partial.shape[0] // len(CHAINS)
    pieces = []
    for piece, steps in enumerate(CHAINS):
        block = partial[piece * share : (piece + 1) * share]
        for axis, bit in steps:
            block = halved(block, axis, bit) if axis == "seq" else exchanged(block, axis)
        pieces.append(block)
    weight_grad = jnp.transpose(jnp.concatenate(pieces, axis=0), (1, 2, 0))
    return (trunk_input, input_grad, weight_grad)


def solution(mesh):
    return jax.shard_map(
        shards,
        mesh=mesh,
        in_specs=(P("dp", "seq", None), P(), P("dp", "seq", None)),
        out_specs=(P("dp", None, "seq"), P("dp", "seq", None), P(None, "dp", "seq")),
        check_vma=False,
    )
```

```python
import jax
import jax.numpy as jnp
from jax import lax
from jax.sharding import PartitionSpec as P
import numpy as np

epsilon = 1e-06
root_half = 0.7071067811865476
inv_root_two_pi = 0.3989422804014327


def with_halo(block, sides, width):
    for axis, dim in sides:
        count = lax.axis_size(axis)
        forward = [(i, i + 1) for i in range(count - 1)]
        backward = [(target, source) for source, target in forward]
        low = lax.ppermute(
            lax.slice_in_dim(block, block.shape[dim] - width, None, axis=dim), axis, forward
        )
        high = lax.ppermute(lax.slice_in_dim(block, 0, width, axis=dim), axis, backward)
        block = jnp.concatenate([low, block, high], axis=dim)
    return block


def halved(block, axis, bit, dim):
    count = lax.axis_size(axis)
    partners = [(i, i ^ (1 << bit)) for i in range(count)]
    mine = (lax.axis_index(axis) >> bit) & 1
    half = block.shape[dim] // 2
    keep = lax.dynamic_slice_in_dim(block, mine * half, half, axis=dim)
    send = lax.dynamic_slice_in_dim(block, (1 - mine) * half, half, axis=dim)
    return keep + lax.ppermute(send, axis, partners)


def picked(block, bits, pieces, piece):
    width = block.shape[-1] // (16 * pieces)
    sources = []
    for place in range(16 * width):
        code, rest = divmod(place, width)
        index = 0
        for step, bit in enumerate(bits):
            index |= ((code >> (3 - step)) & 1) << bit
        sources.append((index * pieces + piece) * width + rest)
    rows = lax.broadcasted_iota(jnp.int32, (block.shape[-1], len(sources)), 0)
    one_hot = (rows == jnp.asarray(np.array(sources, np.int32))[None, :]).astype(block.dtype)
    moved = jnp.einsum("blc,co->blo", block, one_hot, preferred_element_type=jnp.float32)
    return moved.astype(block.dtype)


CHAINS = (
    (("seq", 0), ("seq", 2), ("seq", 1), ("dp", 0), ("seq", 3), ("dp", 3), ("dp", 1), ("dp", 2)),
    (("seq", 0), ("seq", 1), ("dp", 0), ("seq", 2), ("seq", 3), ("dp", 3), ("dp", 1), ("dp", 2)),
    (("seq", 0), ("dp", 0), ("seq", 2), ("seq", 1), ("seq", 3), ("dp", 3), ("dp", 1), ("dp", 2)),
)


def gaussian_unit(value):
    return 0.5 * value * (1.0 + jax.scipy.special.erf(value * root_half))


def gaussian_slope(value):
    return 0.5 * (
        1.0 + jax.scipy.special.erf(value * root_half)
    ) + value * inv_root_two_pi * jnp.exp(-0.5 * value * value)


def windows(padded, length, taps):
    return jnp.stack([padded[:, offset : offset + length] for offset in range(taps)], axis=2)


def shards(features, weight, cotangent):
    taps = weight.shape[0]
    channels = weight.shape[2]
    batch = features.shape[0]
    length = features.shape[1]
    reach = taps // 2
    floats = features.astype(jnp.float32)
    inverse = lax.rsqrt(jnp.mean(floats * floats, axis=-1, keepdims=True) + epsilon)
    normed = floats * inverse
    activations = gaussian_unit(normed).astype(jnp.bfloat16)
    halves = 0.5 * cotangent.astype(jnp.float32)
    upward = jnp.broadcast_to(halves[:, :, None, :], (batch, length // 2, 2, channels)).reshape(
        batch, length, channels
    )
    branch_grad = upward.astype(jnp.bfloat16)
    padded_acts = with_halo(activations, (("seq", 1),), reach)
    padded_grad = with_halo(branch_grad, (("seq", 1),), reach)
    grad_window = jnp.stack(
        [padded_grad[:, taps - 1 - k : taps - 1 - k + length] for k in range(taps)], axis=2
    )
    act_grad = jnp.einsum("blko,kio->bli", grad_window, weight, preferred_element_type=jnp.float32)
    slope_grad = act_grad * gaussian_slope(normed)
    centred = jnp.mean(slope_grad * floats, axis=-1, keepdims=True)
    input_grad = (upward + inverse * slope_grad - floats * inverse**3 * centred).astype(
        jnp.bfloat16
    )
    dp_order = tuple(bit for axis, bit in CHAINS[0] if axis == "dp")
    act_window = windows(picked(padded_acts, dp_order, 1, 0), length, taps)
    shares = []
    for piece, steps in enumerate(CHAINS):
        seq_order = tuple(bit for axis, bit in steps if axis == "seq")
        shares.append(
            jnp.einsum(
                "blo,blki->oki",
                picked(branch_grad, seq_order, len(CHAINS), piece),
                act_window,
                preferred_element_type=jnp.float32,
            )
        )
    for step in range(len(CHAINS[0])):
        for piece, steps in enumerate(CHAINS):
            axis, bit = steps[step]
            shares[piece] = halved(shares[piece], axis, bit, 0 if axis == "seq" else 2)
        if step == 0:
            shares, padded_acts, floats = lax.optimization_barrier((shares, padded_acts, floats))
    weight_grad = jnp.transpose(jnp.concatenate(shares, axis=0), (1, 2, 0))
    window = windows(padded_acts, length, taps)
    mixed = jnp.einsum("blki,kio->blo", window, weight, preferred_element_type=jnp.float32)
    summed = floats + mixed
    paired = summed.reshape(batch, length // 2, 2, channels)
    pooled = (0.5 * (paired[:, :, 0] + paired[:, :, 1])).astype(jnp.bfloat16)
    trunk_input = lax.all_to_all(pooled, "seq", split_axis=2, concat_axis=1, tiled=True)
    return (trunk_input, input_grad, weight_grad)


def solution(mesh):
    return jax.shard_map(
        shards,
        mesh=mesh,
        in_specs=(P("dp", "seq", None), P(), P("dp", "seq", None)),
        out_specs=(P("dp", None, "seq"), P("dp", "seq", None), P(None, "dp", "seq")),
        check_vma=False,
    )
```

```python
import jax
import jax.numpy as jnp
from jax import lax
from jax.sharding import PartitionSpec as P
import numpy as np

epsilon = 1e-06
root_half = 0.7071067811865476
inv_root_two_pi = 0.3989422804014327


def with_halo(block, sides, width):
    for axis, dim in sides:
        count = lax.axis_size(axis)
        forward = [(i, i + 1) for i in range(count - 1)]
        backward = [(target, source) for source, target in forward]
        low = lax.ppermute(
            lax.slice_in_dim(block, block.shape[dim] - width, None, axis=dim), axis, forward
        )
        high = lax.ppermute(lax.slice_in_dim(block, 0, width, axis=dim), axis, backward)
        block = jnp.concatenate([low, block, high], axis=dim)
    return block


def halved(block, axis, bit, dim):
    count = lax.axis_size(axis)
    partners = [(i, i ^ (1 << bit)) for i in range(count)]
    mine = (lax.axis_index(axis) >> bit) & 1
    half = block.shape[dim] // 2
    keep = lax.dynamic_slice_in_dim(block, mine * half, half, axis=dim)
    send = lax.dynamic_slice_in_dim(block, (1 - mine) * half, half, axis=dim)
    return keep + lax.ppermute(send, axis, partners)


def picked(block, bits, pieces, piece):
    width = block.shape[-1] // (16 * pieces)
    sources = []
    for place in range(16 * width):
        code, rest = divmod(place, width)
        index = 0
        for step, bit in enumerate(bits):
            index |= ((code >> (3 - step)) & 1) << bit
        sources.append((index * pieces + piece) * width + rest)
    rows = lax.broadcasted_iota(jnp.int32, (block.shape[-1], len(sources)), 0)
    one_hot = (rows == jnp.asarray(np.array(sources, np.int32))[None, :]).astype(block.dtype)
    moved = jnp.einsum("blc,co->blo", block, one_hot, preferred_element_type=jnp.float32)
    return moved.astype(block.dtype)


CHAINS = (
    (("seq", 0), ("seq", 2), ("seq", 1), ("dp", 0), ("seq", 3), ("dp", 3), ("dp", 1), ("dp", 2)),
    (("seq", 0), ("seq", 1), ("dp", 0), ("seq", 2), ("seq", 3), ("dp", 3), ("dp", 1), ("dp", 2)),
    (("seq", 0), ("dp", 0), ("seq", 2), ("seq", 1), ("seq", 3), ("dp", 3), ("dp", 1), ("dp", 2)),
)


def gaussian_unit(value):
    return 0.5 * value * (1.0 + jax.scipy.special.erf(value * root_half))


def gaussian_slope(value):
    return 0.5 * (
        1.0 + jax.scipy.special.erf(value * root_half)
    ) + value * inv_root_two_pi * jnp.exp(-0.5 * value * value)


def windows(padded, length, taps):
    return jnp.stack([padded[:, offset : offset + length] for offset in range(taps)], axis=2)


def shards(features, weight, cotangent):
    taps = weight.shape[0]
    channels = weight.shape[2]
    batch = features.shape[0]
    length = features.shape[1]
    reach = taps // 2
    floats = features.astype(jnp.float32)
    inverse = lax.rsqrt(jnp.mean(floats * floats, axis=-1, keepdims=True) + epsilon)
    normed = floats * inverse
    activations = gaussian_unit(normed).astype(jnp.bfloat16)
    halves = 0.5 * cotangent.astype(jnp.float32)
    upward = jnp.broadcast_to(halves[:, :, None, :], (batch, length // 2, 2, channels)).reshape(
        batch, length, channels
    )
    branch_grad = upward.astype(jnp.bfloat16)
    padded_acts = with_halo(activations, (("seq", 1),), reach)
    padded_grad = with_halo(branch_grad, (("seq", 1),), reach)
    grad_window = jnp.stack(
        [padded_grad[:, taps - 1 - k : taps - 1 - k + length] for k in range(taps)], axis=2
    )
    act_grad = jnp.einsum("blko,kio->bli", grad_window, weight, preferred_element_type=jnp.float32)
    slope_grad = act_grad * gaussian_slope(normed)
    centred = jnp.mean(slope_grad * floats, axis=-1, keepdims=True)
    input_grad = (upward + inverse * slope_grad - floats * inverse**3 * centred).astype(
        jnp.bfloat16
    )
    dp_order = tuple(bit for axis, bit in CHAINS[0] if axis == "dp")
    act_window = windows(picked(padded_acts, dp_order, 1, 0), length, taps)
    columns = jnp.concatenate(
        [
            picked(branch_grad, tuple(bit for axis, bit in steps if axis == "seq"), len(CHAINS), piece)
            for piece, steps in enumerate(CHAINS)
        ],
        axis=-1,
    )
    partial = jnp.einsum("blo,blki->oki", columns, act_window, preferred_element_type=jnp.float32)
    partial = partial.reshape((len(CHAINS), -1) + partial.shape[1:])
    shared = [step for step in range(len(CHAINS[0])) if len({steps[step] for steps in CHAINS}) == 1]
    for step in range(len(CHAINS[0])):
        if step in shared:
            if isinstance(partial, list):
                partial = jnp.stack(partial)
            axis, bit = CHAINS[0][step]
            partial = halved(partial, axis, bit, 1 if axis == "seq" else 3)
        else:
            partial = [
                halved(partial[piece], axis, bit, 0 if axis == "seq" else 2)
                for piece, (axis, bit) in enumerate(steps[step] for steps in CHAINS)
            ]
        if step == 0:
            partial, padded_acts, floats = lax.optimization_barrier((partial, padded_acts, floats))
    weight_grad = jnp.transpose(partial.reshape((-1,) + partial.shape[2:]), (1, 2, 0))
    window = windows(padded_acts, length, taps)
    mixed = jnp.einsum("blki,kio->blo", window, weight, preferred_element_type=jnp.float32)
    summed = floats + mixed
    paired = summed.reshape(batch, length // 2, 2, channels)
    pooled = (0.5 * (paired[:, :, 0] + paired[:, :, 1])).astype(jnp.bfloat16)
    trunk_input = lax.all_to_all(pooled, "seq", split_axis=2, concat_axis=1, tiled=True)
    return (trunk_input, input_grad, weight_grad)


def solution(mesh):
    return jax.shard_map(
        shards,
        mesh=mesh,
        in_specs=(P("dp", "seq", None), P(), P("dp", "seq", None)),
        out_specs=(P("dp", None, "seq"), P("dp", "seq", None), P(None, "dp", "seq")),
        check_vma=False,
    )
```

```python
import jax
import jax.numpy as jnp
from jax import lax
from jax.sharding import PartitionSpec as P
import numpy as np

epsilon = 1e-06
root_half = 0.7071067811865476
inv_root_two_pi = 0.3989422804014327


def with_halo(block, sides, width):
    for axis, dim in sides:
        count = lax.axis_size(axis)
        forward = [(i, i + 1) for i in range(count - 1)]
        backward = [(target, source) for source, target in forward]
        low = lax.ppermute(
            lax.slice_in_dim(block, block.shape[dim] - width, None, axis=dim), axis, forward
        )
        high = lax.ppermute(lax.slice_in_dim(block, 0, width, axis=dim), axis, backward)
        block = jnp.concatenate([low, block, high], axis=dim)
    return block


def halved(block, axis, bit, dim):
    count = lax.axis_size(axis)
    partners = [(i, i ^ (1 << bit)) for i in range(count)]
    mine = (lax.axis_index(axis) >> bit) & 1
    half = block.shape[dim] // 2
    keep = lax.dynamic_slice_in_dim(block, mine * half, half, axis=dim)
    send = lax.dynamic_slice_in_dim(block, (1 - mine) * half, half, axis=dim)
    return keep + lax.ppermute(send, axis, partners)


def sources_of(channels, orders):
    pieces = len(orders)
    width = channels // (16 * pieces)
    sources = []
    for piece, bits in enumerate(orders):
        for place in range(16 * width):
            code, rest = divmod(place, width)
            index = 0
            for step, bit in enumerate(bits):
                index |= ((code >> (len(bits) - 1 - step)) & 1) << bit
            sources.append((index * pieces + piece) * width + rest)
    return np.array(sources, np.int32)


def picked(block, sources):
    rows = lax.broadcasted_iota(jnp.int32, (block.shape[-1], sources.shape[0]), 0)
    one_hot = (rows == sources[None, :]).astype(block.dtype)
    moved = jnp.einsum("blc,co->blo", block, one_hot, preferred_element_type=jnp.float32)
    return moved.astype(block.dtype)


CHAINS = (
    (("seq", 0), ("seq", 2), ("seq", 1), ("dp", 0), ("seq", 3), ("dp", 3), ("dp", 1), ("dp", 2)),
    (("seq", 0), ("seq", 1), ("dp", 0), ("seq", 2), ("seq", 3), ("dp", 3), ("dp", 1), ("dp", 2)),
    (("seq", 0), ("dp", 0), ("seq", 2), ("seq", 1), ("seq", 3), ("dp", 3), ("dp", 1), ("dp", 2)),
)


def gaussian_unit(value):
    return 0.5 * value * (1.0 + jax.scipy.special.erf(value * root_half))


def gaussian_slope(value):
    return 0.5 * (
        1.0 + jax.scipy.special.erf(value * root_half)
    ) + value * inv_root_two_pi * jnp.exp(-0.5 * value * value)


def windows(padded, length, taps):
    return jnp.stack([padded[:, offset : offset + length] for offset in range(taps)], axis=2)


def shards(features, weight, cotangent):
    taps = weight.shape[0]
    channels = weight.shape[2]
    batch = features.shape[0]
    length = features.shape[1]
    reach = taps // 2
    floats = features.astype(jnp.float32)
    inverse = lax.rsqrt(jnp.mean(floats * floats, axis=-1, keepdims=True) + epsilon)
    normed = floats * inverse
    activations = gaussian_unit(normed).astype(jnp.bfloat16)
    halves = 0.5 * cotangent.astype(jnp.float32)
    upward = jnp.broadcast_to(halves[:, :, None, :], (batch, length // 2, 2, channels)).reshape(
        batch, length, channels
    )
    branch_grad = upward.astype(jnp.bfloat16)
    padded_acts = with_halo(activations, (("seq", 1),), reach)
    padded_grad = with_halo(branch_grad, (("seq", 1),), reach)
    grad_window = jnp.stack(
        [padded_grad[:, taps - 1 - k : taps - 1 - k + length] for k in range(taps)], axis=2
    )
    act_grad = jnp.einsum("blko,kio->bli", grad_window, weight, preferred_element_type=jnp.float32)
    slope_grad = act_grad * gaussian_slope(normed)
    centred = jnp.mean(slope_grad * floats, axis=-1, keepdims=True)
    input_grad = (upward + inverse * slope_grad - floats * inverse**3 * centred).astype(
        jnp.bfloat16
    )
    dp_order = tuple(bit for axis, bit in CHAINS[0] if axis == "dp")
    act_window = windows(
        picked(padded_acts, jnp.asarray(sources_of(padded_acts.shape[-1], (dp_order,)))), length, taps
    )
    orders = [tuple(bit for axis, bit in steps if axis == "seq") for steps in CHAINS]
    columns = jnp.asarray(sources_of(channels, orders)).reshape(len(CHAINS), 2, -1)
    axis, bit = CHAINS[0][0]
    mine = (lax.axis_index(axis) >> bit) & 1
    halves = []
    for side in (mine, 1 - mine):
        chosen = lax.dynamic_index_in_dim(columns, side, axis=1, keepdims=False).reshape(-1)
        product = jnp.einsum(
            "blo,blki->oki", picked(branch_grad, chosen), act_window, preferred_element_type=jnp.float32
        )
        halves.append(product.reshape((len(CHAINS), -1) + product.shape[1:]))
    partners = [(i, i ^ (1 << bit)) for i in range(lax.axis_size(axis))]
    partial = halves[0] + lax.ppermute(halves[1], axis, partners)
    partial, padded_acts, floats = lax.optimization_barrier((partial, padded_acts, floats))
    shared = [step for step in range(len(CHAINS[0])) if len({steps[step] for steps in CHAINS}) == 1]
    for step in range(1, len(CHAINS[0])):
        if step in shared:
            if isinstance(partial, list):
                partial = jnp.stack(partial)
            axis, bit = CHAINS[0][step]
            partial = halved(partial, axis, bit, 1 if axis == "seq" else 3)
        else:
            partial = [
                halved(partial[piece], axis, bit, 0 if axis == "seq" else 2)
                for piece, (axis, bit) in enumerate(steps[step] for steps in CHAINS)
            ]
    weight_grad = jnp.transpose(partial.reshape((-1,) + partial.shape[2:]), (1, 2, 0))
    window = windows(padded_acts, length, taps)
    mixed = jnp.einsum("blki,kio->blo", window, weight, preferred_element_type=jnp.float32)
    summed = floats + mixed
    paired = summed.reshape(batch, length // 2, 2, channels)
    pooled = (0.5 * (paired[:, :, 0] + paired[:, :, 1])).astype(jnp.bfloat16)
    trunk_input = lax.all_to_all(pooled, "seq", split_axis=2, concat_axis=1, tiled=True)
    return (trunk_input, input_grad, weight_grad)


def solution(mesh):
    return jax.shard_map(
        shards,
        mesh=mesh,
        in_specs=(P("dp", "seq", None), P(), P("dp", "seq", None)),
        out_specs=(P("dp", None, "seq"), P("dp", "seq", None), P(None, "dp", "seq")),
        check_vma=False,
    )
```

```python
import jax
import jax.numpy as jnp
from jax import lax
from jax.sharding import PartitionSpec as P
import numpy as np

epsilon = 1e-06
root_half = 0.7071067811865476
inv_root_two_pi = 0.3989422804014327


def with_halo(block, sides, width):
    for axis, dim in sides:
        count = lax.axis_size(axis)
        forward = [(i, i + 1) for i in range(count - 1)]
        backward = [(target, source) for source, target in forward]
        low = lax.ppermute(
            lax.slice_in_dim(block, block.shape[dim] - width, None, axis=dim), axis, forward
        )
        high = lax.ppermute(lax.slice_in_dim(block, 0, width, axis=dim), axis, backward)
        block = jnp.concatenate([low, block, high], axis=dim)
    return block


def halved(block, axis, bit, dim):
    count = lax.axis_size(axis)
    partners = [(i, i ^ (1 << bit)) for i in range(count)]
    mine = (lax.axis_index(axis) >> bit) & 1
    half = block.shape[dim] // 2
    keep = lax.dynamic_slice_in_dim(block, mine * half, half, axis=dim)
    send = lax.dynamic_slice_in_dim(block, (1 - mine) * half, half, axis=dim)
    return keep + lax.ppermute(send, axis, partners)


def sources_of(channels, orders):
    pieces = len(orders)
    width = channels // (16 * pieces)
    sources = []
    for piece, bits in enumerate(orders):
        for place in range(16 * width):
            code, rest = divmod(place, width)
            index = 0
            for step, bit in enumerate(bits):
                index |= ((code >> (len(bits) - 1 - step)) & 1) << bit
            sources.append((index * pieces + piece) * width + rest)
    return np.array(sources, np.int32)


def picked(block, sources):
    rows = lax.broadcasted_iota(jnp.int32, (block.shape[-1], sources.shape[0]), 0)
    one_hot = (rows == sources[None, :]).astype(block.dtype)
    moved = jnp.einsum("blc,co->blo", block, one_hot, preferred_element_type=jnp.float32)
    return moved.astype(block.dtype)


CHAINS = (
    (("seq", 0), ("seq", 2), ("seq", 1), ("dp", 0), ("seq", 3), ("dp", 3), ("dp", 1), ("dp", 2)),
    (("seq", 0), ("seq", 1), ("dp", 0), ("seq", 2), ("seq", 3), ("dp", 3), ("dp", 1), ("dp", 2)),
    (("seq", 0), ("dp", 0), ("seq", 2), ("seq", 1), ("seq", 3), ("dp", 3), ("dp", 1), ("dp", 2)),
)


def gaussian_unit(value):
    return 0.5 * value * (1.0 + jax.scipy.special.erf(value * root_half))


def gaussian_slope(value):
    return 0.5 * (
        1.0 + jax.scipy.special.erf(value * root_half)
    ) + value * inv_root_two_pi * jnp.exp(-0.5 * value * value)


def windows(padded, length, taps):
    return jnp.stack([padded[:, offset : offset + length] for offset in range(taps)], axis=2)


def shards(features, weight, cotangent):
    taps = weight.shape[0]
    channels = weight.shape[2]
    batch = features.shape[0]
    length = features.shape[1]
    reach = taps // 2
    floats = features.astype(jnp.float32)
    inverse = lax.rsqrt(jnp.mean(floats * floats, axis=-1, keepdims=True) + epsilon)
    normed = floats * inverse
    activations = gaussian_unit(normed).astype(jnp.bfloat16)
    spread = (
        lax.broadcasted_iota(jnp.int32, (length, length // 2), 0) // 2
        == lax.broadcasted_iota(jnp.int32, (length, length // 2), 1)
    ).astype(cotangent.dtype)
    upward = 0.5 * jnp.einsum("bjc,lj->blc", cotangent, spread, preferred_element_type=jnp.float32)
    branch_grad = upward.astype(jnp.bfloat16)
    padded_acts = with_halo(activations, (("seq", 1),), reach)
    padded_grad = with_halo(branch_grad, (("seq", 1),), reach)
    dp_order = tuple(bit for axis, bit in CHAINS[0] if axis == "dp")
    act_window = windows(
        picked(padded_acts, jnp.asarray(sources_of(padded_acts.shape[-1], (dp_order,)))), length, taps
    )
    orders = [tuple(bit for axis, bit in steps if axis == "seq") for steps in CHAINS]
    columns = jnp.asarray(sources_of(channels, orders)).reshape(len(CHAINS), 2, -1)
    axis, bit = CHAINS[0][0]
    mine = (lax.axis_index(axis) >> bit) & 1
    halves = []
    for side in (mine, 1 - mine):
        chosen = lax.dynamic_index_in_dim(columns, side, axis=1, keepdims=False).reshape(-1)
        product = jnp.einsum(
            "blo,blki->oki", picked(branch_grad, chosen), act_window, preferred_element_type=jnp.float32
        )
        halves.append(product.reshape((len(CHAINS), -1) + product.shape[1:]))
    partners = [(i, i ^ (1 << bit)) for i in range(lax.axis_size(axis))]
    partial = halves[0] + lax.ppermute(halves[1], axis, partners)
    partial, padded_acts, padded_grad, floats, upward = lax.optimization_barrier(
        (partial, padded_acts, padded_grad, floats, upward)
    )
    inverse = lax.rsqrt(jnp.mean(floats * floats, axis=-1, keepdims=True) + epsilon)
    normed = floats * inverse
    grad_window = jnp.stack(
        [padded_grad[:, taps - 1 - k : taps - 1 - k + length] for k in range(taps)], axis=2
    )
    act_grad = jnp.einsum("blko,kio->bli", grad_window, weight, preferred_element_type=jnp.float32)
    slope_grad = act_grad * gaussian_slope(normed)
    centred = jnp.mean(slope_grad * floats, axis=-1, keepdims=True)
    input_grad = (upward + inverse * slope_grad - floats * inverse**3 * centred).astype(
        jnp.bfloat16
    )
    shared = [step for step in range(len(CHAINS[0])) if len({steps[step] for steps in CHAINS}) == 1]
    for step in range(1, len(CHAINS[0])):
        if step in shared:
            if isinstance(partial, list):
                partial = jnp.stack(partial)
            axis, bit = CHAINS[0][step]
            partial = halved(partial, axis, bit, 1 if axis == "seq" else 3)
        else:
            partial = [
                halved(partial[piece], axis, bit, 0 if axis == "seq" else 2)
                for piece, (axis, bit) in enumerate(steps[step] for steps in CHAINS)
            ]
    weight_grad = jnp.transpose(partial.reshape((-1,) + partial.shape[2:]), (1, 2, 0))
    window = windows(padded_acts, length, taps)
    mixed = jnp.einsum("blki,kio->blo", window, weight, preferred_element_type=jnp.float32)
    summed = floats + mixed
    paired = summed.reshape(batch, length // 2, 2, channels)
    pooled = (0.5 * (paired[:, :, 0] + paired[:, :, 1])).astype(jnp.bfloat16)
    trunk_input = lax.all_to_all(pooled, "seq", split_axis=2, concat_axis=1, tiled=True)
    return (trunk_input, input_grad, weight_grad)


def solution(mesh):
    return jax.shard_map(
        shards,
        mesh=mesh,
        in_specs=(P("dp", "seq", None), P(), P("dp", "seq", None)),
        out_specs=(P("dp", None, "seq"), P("dp", "seq", None), P(None, "dp", "seq")),
        check_vma=False,
    )
```

```python
import jax
import jax.numpy as jnp
from jax import lax
from jax.sharding import PartitionSpec as P
import numpy as np

epsilon = 1e-06
root_half = 0.7071067811865476
inv_root_two_pi = 0.3989422804014327


def with_halo(block, sides, width):
    for axis, dim in sides:
        count = lax.axis_size(axis)
        forward = [(i, i + 1) for i in range(count - 1)]
        backward = [(target, source) for source, target in forward]
        low = lax.ppermute(
            lax.slice_in_dim(block, block.shape[dim] - width, None, axis=dim), axis, forward
        )
        high = lax.ppermute(lax.slice_in_dim(block, 0, width, axis=dim), axis, backward)
        block = jnp.concatenate([low, block, high], axis=dim)
    return block


def halved(block, axis, bit, dim):
    count = lax.axis_size(axis)
    partners = [(i, i ^ (1 << bit)) for i in range(count)]
    mine = (lax.axis_index(axis) >> bit) & 1
    half = block.shape[dim] // 2
    keep = lax.dynamic_slice_in_dim(block, mine * half, half, axis=dim)
    send = lax.dynamic_slice_in_dim(block, (1 - mine) * half, half, axis=dim)
    return keep + lax.ppermute(send, axis, partners)


def sources_of(channels, orders):
    pieces = len(orders)
    width = channels // (16 * pieces)
    sources = []
    for piece, bits in enumerate(orders):
        for place in range(16 * width):
            code, rest = divmod(place, width)
            index = 0
            for step, bit in enumerate(bits):
                index |= ((code >> (len(bits) - 1 - step)) & 1) << bit
            sources.append((index * pieces + piece) * width + rest)
    return np.array(sources, np.int32)


def picked(block, sources):
    rows = lax.broadcasted_iota(jnp.int32, (block.shape[-1], sources.shape[0]), 0)
    one_hot = (rows == sources[None, :]).astype(block.dtype)
    moved = jnp.einsum("blc,co->blo", block, one_hot, preferred_element_type=jnp.float32)
    return moved.astype(block.dtype)


CHAINS = (
    (("seq", 0), ("seq", 2), ("seq", 1), ("dp", 0), ("seq", 3), ("dp", 3), ("dp", 1), ("dp", 2)),
    (("seq", 0), ("seq", 1), ("dp", 0), ("seq", 2), ("seq", 3), ("dp", 3), ("dp", 1), ("dp", 2)),
    (("seq", 0), ("dp", 0), ("seq", 2), ("seq", 1), ("seq", 3), ("dp", 3), ("dp", 1), ("dp", 2)),
)


def gaussian_unit(value):
    return 0.5 * value * (1.0 + jax.scipy.special.erf(value * root_half))


def gaussian_slope(value):
    return 0.5 * (
        1.0 + jax.scipy.special.erf(value * root_half)
    ) + value * inv_root_two_pi * jnp.exp(-0.5 * value * value)


def windows(padded, length, taps):
    return jnp.stack([padded[:, offset : offset + length] for offset in range(taps)], axis=2)


def shards(features, weight, cotangent):
    taps = weight.shape[0]
    channels = weight.shape[2]
    batch = features.shape[0]
    length = features.shape[1]
    reach = taps // 2
    floats = features.astype(jnp.float32)
    inverse = lax.rsqrt(jnp.mean(floats * floats, axis=-1, keepdims=True) + epsilon)
    normed = floats * inverse
    activations = gaussian_unit(normed).astype(jnp.bfloat16)
    spread = (
        lax.broadcasted_iota(jnp.int32, (length, length // 2), 0) // 2
        == lax.broadcasted_iota(jnp.int32, (length, length // 2), 1)
    ).astype(cotangent.dtype)
    upward = 0.5 * jnp.einsum("bjc,lj->blc", cotangent, spread, preferred_element_type=jnp.float32)
    branch_grad = upward.astype(jnp.bfloat16)
    padded_acts = with_halo(activations, (("seq", 1),), reach)
    padded_grad = with_halo(branch_grad, (("seq", 1),), reach)
    dp_order = tuple(bit for axis, bit in CHAINS[0] if axis == "dp")
    act_window = windows(
        picked(padded_acts, jnp.asarray(sources_of(padded_acts.shape[-1], (dp_order,)))), length, taps
    )
    orders = [tuple(bit for axis, bit in steps if axis == "seq") for steps in CHAINS]
    columns = jnp.asarray(sources_of(channels, orders)).reshape(len(CHAINS), 2, -1)
    axis, bit = CHAINS[0][0]
    mine = (lax.axis_index(axis) >> bit) & 1
    halves = []
    for side in (mine, 1 - mine):
        chosen = lax.dynamic_index_in_dim(columns, side, axis=1, keepdims=False).reshape(-1)
        product = jnp.einsum(
            "blo,blki->oki", picked(branch_grad, chosen), act_window, preferred_element_type=jnp.float32
        )
        halves.append(product)
    partners = [(i, i ^ (1 << bit)) for i in range(lax.axis_size(axis))]
    partial = halves[0] + lax.ppermute(halves[1], axis, partners)
    partial = partial.reshape((len(CHAINS), -1) + partial.shape[1:])
    partial, padded_acts, padded_grad, floats, upward = lax.optimization_barrier(
        (partial, padded_acts, padded_grad, floats, upward)
    )
    inverse = lax.rsqrt(jnp.mean(floats * floats, axis=-1, keepdims=True) + epsilon)
    normed = floats * inverse
    grad_window = jnp.stack(
        [padded_grad[:, taps - 1 - k : taps - 1 - k + length] for k in range(taps)], axis=2
    )
    act_grad = jnp.einsum("blko,kio->bli", grad_window, weight, preferred_element_type=jnp.float32)
    slope_grad = act_grad * gaussian_slope(normed)
    centred = jnp.mean(slope_grad * floats, axis=-1, keepdims=True)
    input_grad = (upward + inverse * slope_grad - floats * inverse**3 * centred).astype(
        jnp.bfloat16
    )
    window = windows(padded_acts, length, taps)
    mixed = jnp.einsum("blki,kio->blo", window, weight, preferred_element_type=jnp.float32)
    summed = floats + mixed
    paired = summed.reshape(batch, length // 2, 2, channels)
    pooled = (0.5 * (paired[:, :, 0] + paired[:, :, 1])).astype(jnp.bfloat16)
    trunk_input = lax.all_to_all(pooled, "seq", split_axis=2, concat_axis=1, tiled=True)
    shared = [step for step in range(len(CHAINS[0])) if len({steps[step] for steps in CHAINS}) == 1]
    for step in range(1, len(CHAINS[0])):
        if step in shared:
            if isinstance(partial, list):
                partial, trunk_input = lax.optimization_barrier((jnp.stack(partial), trunk_input))
            axis, bit = CHAINS[0][step]
            partial = halved(partial, axis, bit, 1 if axis == "seq" else 3)
        else:
            partial = [
                halved(partial[piece], axis, bit, 0 if axis == "seq" else 2)
                for piece, (axis, bit) in enumerate(steps[step] for steps in CHAINS)
            ]
    weight_grad = jnp.transpose(partial.reshape((-1,) + partial.shape[2:]), (1, 2, 0))
    return (trunk_input, input_grad, weight_grad)


def solution(mesh):
    return jax.shard_map(
        shards,
        mesh=mesh,
        in_specs=(P("dp", "seq", None), P(), P("dp", "seq", None)),
        out_specs=(P("dp", None, "seq"), P("dp", "seq", None), P(None, "dp", "seq")),
        check_vma=False,
    )
```

```python
import jax
import jax.numpy as jnp
from jax import lax
from jax.sharding import PartitionSpec as P
import numpy as np

epsilon = 1e-06
root_half = 0.7071067811865476
inv_root_two_pi = 0.3989422804014327


def with_halo(block, sides, width):
    for axis, dim in sides:
        count = lax.axis_size(axis)
        forward = [(i, i + 1) for i in range(count - 1)]
        backward = [(target, source) for source, target in forward]
        low = lax.ppermute(
            lax.slice_in_dim(block, block.shape[dim] - width, None, axis=dim), axis, forward
        )
        high = lax.ppermute(lax.slice_in_dim(block, 0, width, axis=dim), axis, backward)
        block = jnp.concatenate([low, block, high], axis=dim)
    return block


def halved(block, axis, bit, dim):
    count = lax.axis_size(axis)
    partners = [(i, i ^ (1 << bit)) for i in range(count)]
    mine = (lax.axis_index(axis) >> bit) & 1
    half = block.shape[dim] // 2
    keep = lax.dynamic_slice_in_dim(block, mine * half, half, axis=dim)
    send = lax.dynamic_slice_in_dim(block, (1 - mine) * half, half, axis=dim)
    return keep + lax.ppermute(send, axis, partners)


def quartered(block, first, second):
    sizes = {axis: lax.axis_size(axis) for axis in ("seq", "dp")}
    bits = [(lax.axis_index(axis) >> bit) & 1 for axis, bit, _ in (first, second)]

    def part(flip_a, flip_b):
        piece = block
        for (axis, bit, dim), mine, flip in zip((first, second), bits, (flip_a, flip_b)):
            half = piece.shape[dim] // 2
            piece = lax.dynamic_slice_in_dim(piece, (mine ^ flip) * half, half, axis=dim)
        return piece

    total = part(0, 0)
    for flip_a, flip_b in ((1, 0), (0, 1), (1, 1)):
        names, pairs = [], None
        for (axis, bit, _), flip in zip((first, second), (flip_a, flip_b)):
            if flip:
                names.append((axis, bit))
        if len(names) == 1 or names[0][0] == names[1][0]:
            axis = names[0][0]
            mask = sum(1 << bit for _, bit in names)
            pairs = [(i, i ^ mask) for i in range(sizes[axis])]
            total = total + lax.ppermute(part(flip_a, flip_b), axis, pairs)
        else:
            (axis_a, bit_a), (axis_b, bit_b) = names
            count_b = sizes[axis_b]
            pairs = [
                (a * count_b + b, (a ^ (1 << bit_a)) * count_b + (b ^ (1 << bit_b)))
                for a in range(sizes[axis_a])
                for b in range(count_b)
            ]
            total = total + lax.ppermute(part(flip_a, flip_b), (axis_a, axis_b), pairs)
    return total


def sources_of(channels, orders):
    pieces = len(orders)
    width = channels // (16 * pieces)
    sources = []
    for piece, bits in enumerate(orders):
        for place in range(16 * width):
            code, rest = divmod(place, width)
            index = 0
            for step, bit in enumerate(bits):
                index |= ((code >> (len(bits) - 1 - step)) & 1) << bit
            sources.append((index * pieces + piece) * width + rest)
    return np.array(sources, np.int32)


def picked(block, sources):
    rows = lax.broadcasted_iota(jnp.int32, (block.shape[-1], sources.shape[0]), 0)
    one_hot = (rows == sources[None, :]).astype(block.dtype)
    moved = jnp.einsum("blc,co->blo", block, one_hot, preferred_element_type=jnp.float32)
    return moved.astype(block.dtype)


CHAINS = (
    (("seq", 0), ("seq", 2), ("seq", 1), ("dp", 0), ("seq", 3), ("dp", 3), ("dp", 1), ("dp", 2)),
    (("seq", 0), ("seq", 1), ("dp", 0), ("seq", 2), ("seq", 3), ("dp", 3), ("dp", 1), ("dp", 2)),
    (("seq", 0), ("dp", 0), ("seq", 2), ("seq", 1), ("seq", 3), ("dp", 3), ("dp", 1), ("dp", 2)),
)


def gaussian_unit(value):
    return 0.5 * value * (1.0 + jax.scipy.special.erf(value * root_half))


def gaussian_slope(value):
    return 0.5 * (
        1.0 + jax.scipy.special.erf(value * root_half)
    ) + value * inv_root_two_pi * jnp.exp(-0.5 * value * value)


def windows(padded, length, taps):
    return jnp.stack([padded[:, offset : offset + length] for offset in range(taps)], axis=2)


def shards(features, weight, cotangent):
    taps = weight.shape[0]
    channels = weight.shape[2]
    batch = features.shape[0]
    length = features.shape[1]
    reach = taps // 2
    floats = features.astype(jnp.float32)
    inverse = lax.rsqrt(jnp.mean(floats * floats, axis=-1, keepdims=True) + epsilon)
    normed = floats * inverse
    activations = gaussian_unit(normed).astype(jnp.bfloat16)
    spread = (
        lax.broadcasted_iota(jnp.int32, (length, length // 2), 0) // 2
        == lax.broadcasted_iota(jnp.int32, (length, length // 2), 1)
    ).astype(cotangent.dtype)
    upward = 0.5 * jnp.einsum("bjc,lj->blc", cotangent, spread, preferred_element_type=jnp.float32)
    branch_grad = upward.astype(jnp.bfloat16)
    padded_acts = with_halo(activations, (("seq", 1),), reach)
    padded_grad = with_halo(branch_grad, (("seq", 1),), reach)
    dp_order = tuple(bit for axis, bit in CHAINS[0] if axis == "dp")
    act_window = windows(
        picked(padded_acts, jnp.asarray(sources_of(padded_acts.shape[-1], (dp_order,)))), length, taps
    )
    orders = [tuple(bit for axis, bit in steps if axis == "seq") for steps in CHAINS]
    columns = jnp.asarray(sources_of(channels, orders)).reshape(len(CHAINS), 2, -1)
    axis, bit = CHAINS[0][0]
    mine = (lax.axis_index(axis) >> bit) & 1
    halves = []
    for side in (mine, 1 - mine):
        chosen = lax.dynamic_index_in_dim(columns, side, axis=1, keepdims=False).reshape(-1)
        product = jnp.einsum(
            "blo,blki->oki", picked(branch_grad, chosen), act_window, preferred_element_type=jnp.float32
        )
        halves.append(product)
    partners = [(i, i ^ (1 << bit)) for i in range(lax.axis_size(axis))]
    partial = halves[0] + lax.ppermute(halves[1], axis, partners)
    partial = partial.reshape((len(CHAINS), -1) + partial.shape[1:])
    partial, padded_acts, padded_grad, floats, upward = lax.optimization_barrier(
        (partial, padded_acts, padded_grad, floats, upward)
    )
    inverse = lax.rsqrt(jnp.mean(floats * floats, axis=-1, keepdims=True) + epsilon)
    normed = floats * inverse
    grad_window = jnp.stack(
        [padded_grad[:, taps - 1 - k : taps - 1 - k + length] for k in range(taps)], axis=2
    )
    act_grad = jnp.einsum("blko,kio->bli", grad_window, weight, preferred_element_type=jnp.float32)
    slope_grad = act_grad * gaussian_slope(normed)
    centred = jnp.mean(slope_grad * floats, axis=-1, keepdims=True)
    input_grad = (upward + inverse * slope_grad - floats * inverse**3 * centred).astype(
        jnp.bfloat16
    )
    window = windows(padded_acts, length, taps)
    mixed = jnp.einsum("blki,kio->blo", window, weight, preferred_element_type=jnp.float32)
    summed = floats + mixed
    paired = summed.reshape(batch, length // 2, 2, channels)
    pooled = (0.5 * (paired[:, :, 0] + paired[:, :, 1])).astype(jnp.bfloat16)
    trunk_input = lax.all_to_all(pooled, "seq", split_axis=2, concat_axis=1, tiled=True)
    shared = [step for step in range(len(CHAINS[0])) if len({steps[step] for steps in CHAINS}) == 1]
    tail = [step for step in shared if step > 0]
    for step in range(1, len(CHAINS[0])):
        if step in tail:
            if isinstance(partial, list):
                partial, trunk_input = lax.optimization_barrier((jnp.stack(partial), trunk_input))
            if (step - tail[0]) % 2 == 0:
                moves = [
                    (axis, bit, 1 if axis == "seq" else 3)
                    for axis, bit in (CHAINS[0][step], CHAINS[0][step + 1])
                ]
                partial = quartered(partial, *moves)
        else:
            partial = [
                halved(partial[piece], axis, bit, 0 if axis == "seq" else 2)
                for piece, (axis, bit) in enumerate(steps[step] for steps in CHAINS)
            ]
    weight_grad = jnp.transpose(partial.reshape((-1,) + partial.shape[2:]), (1, 2, 0))
    return (trunk_input, input_grad, weight_grad)


def solution(mesh):
    return jax.shard_map(
        shards,
        mesh=mesh,
        in_specs=(P("dp", "seq", None), P(), P("dp", "seq", None)),
        out_specs=(P("dp", None, "seq"), P("dp", "seq", None), P(None, "dp", "seq")),
        check_vma=False,
    )
```

```python
import jax
import jax.numpy as jnp
from jax import lax
from jax.sharding import PartitionSpec as P
import numpy as np

epsilon = 1e-06
root_half = 0.7071067811865476
inv_root_two_pi = 0.3989422804014327


def with_halo(block, sides, width):
    for axis, dim in sides:
        count = lax.axis_size(axis)
        forward = [(i, i + 1) for i in range(count - 1)]
        backward = [(target, source) for source, target in forward]
        low = lax.ppermute(
            lax.slice_in_dim(block, block.shape[dim] - width, None, axis=dim), axis, forward
        )
        high = lax.ppermute(lax.slice_in_dim(block, 0, width, axis=dim), axis, backward)
        block = jnp.concatenate([low, block, high], axis=dim)
    return block


def halved(block, axis, bit, dim):
    count = lax.axis_size(axis)
    partners = [(i, i ^ (1 << bit)) for i in range(count)]
    mine = (lax.axis_index(axis) >> bit) & 1
    half = block.shape[dim] // 2
    keep = lax.dynamic_slice_in_dim(block, mine * half, half, axis=dim)
    send = lax.dynamic_slice_in_dim(block, (1 - mine) * half, half, axis=dim)
    return keep + lax.ppermute(send, axis, partners)


def sources_of(channels, orders):
    pieces = len(orders)
    width = channels // (16 * pieces)
    sources = []
    for piece, bits in enumerate(orders):
        for place in range(16 * width):
            code, rest = divmod(place, width)
            index = 0
            for step, bit in enumerate(bits):
                index |= ((code >> (len(bits) - 1 - step)) & 1) << bit
            sources.append((index * pieces + piece) * width + rest)
    return np.array(sources, np.int32)


def picked(block, sources):
    rows = lax.broadcasted_iota(jnp.int32, (block.shape[-1], sources.shape[0]), 0)
    one_hot = (rows == sources[None, :]).astype(block.dtype)
    moved = jnp.einsum("blc,co->blo", block, one_hot, preferred_element_type=jnp.float32)
    return moved.astype(block.dtype)


CHAINS = (
    (("seq", 0), ("seq", 2), ("seq", 1), ("dp", 0), ("seq", 3), ("dp", 3), ("dp", 1), ("dp", 2)),
    (("seq", 0), ("seq", 1), ("dp", 0), ("seq", 2), ("seq", 3), ("dp", 3), ("dp", 1), ("dp", 2)),
    (("seq", 0), ("dp", 0), ("seq", 2), ("seq", 1), ("seq", 3), ("dp", 3), ("dp", 1), ("dp", 2)),
)


def gaussian_unit(value):
    return 0.5 * value * (1.0 + jax.scipy.special.erf(value * root_half))


def gaussian_slope(value):
    return 0.5 * (
        1.0 + jax.scipy.special.erf(value * root_half)
    ) + value * inv_root_two_pi * jnp.exp(-0.5 * value * value)


def windows(padded, length, taps):
    return jnp.stack([padded[:, offset : offset + length] for offset in range(taps)], axis=2)


def shards(features, weight, cotangent):
    taps = weight.shape[0]
    channels = weight.shape[2]
    batch = features.shape[0]
    length = features.shape[1]
    reach = taps // 2
    floats = features.astype(jnp.float32)
    inverse = lax.rsqrt(jnp.mean(floats * floats, axis=-1, keepdims=True) + epsilon)
    normed = floats * inverse
    activations = gaussian_unit(normed).astype(jnp.bfloat16)
    spread = (
        lax.broadcasted_iota(jnp.int32, (length, length // 2), 0) // 2
        == lax.broadcasted_iota(jnp.int32, (length, length // 2), 1)
    ).astype(cotangent.dtype)
    upward = 0.5 * jnp.einsum("bjc,lj->blc", cotangent, spread, preferred_element_type=jnp.float32)
    branch_grad = upward.astype(jnp.bfloat16)
    padded_acts = with_halo(activations, (("seq", 1),), reach)
    padded_grad = with_halo(branch_grad, (("seq", 1),), reach)
    dp_order = tuple(bit for axis, bit in CHAINS[0] if axis == "dp")
    act_window = windows(
        picked(padded_acts, jnp.asarray(sources_of(padded_acts.shape[-1], (dp_order,)))), length, taps
    )
    orders = [tuple(bit for axis, bit in steps if axis == "seq") for steps in CHAINS]
    columns = jnp.asarray(sources_of(channels, orders)).reshape(len(CHAINS), 2, -1)
    axis, bit = CHAINS[0][0]
    mine = (lax.axis_index(axis) >> bit) & 1

    def product(side, grads, acts):
        chosen = lax.dynamic_index_in_dim(columns, side, axis=1, keepdims=False).reshape(-1)
        return jnp.einsum(
            "blo,blki->oki", picked(grads, chosen), acts, preferred_element_type=jnp.float32
        )

    sent = product(1 - mine, branch_grad, act_window)
    sent, forward_acts, forward_floats = lax.optimization_barrier((sent, padded_acts, floats))
    window = windows(forward_acts, length, taps)
    mixed = jnp.einsum("blki,kio->blo", window, weight, preferred_element_type=jnp.float32)
    summed = forward_floats + mixed
    paired = summed.reshape(batch, length // 2, 2, channels)
    pooled = (0.5 * (paired[:, :, 0] + paired[:, :, 1])).astype(jnp.bfloat16)
    trunk_input = lax.all_to_all(pooled, "seq", split_axis=2, concat_axis=1, tiled=True)
    pooled, kept_grads, kept_acts = lax.optimization_barrier((pooled, branch_grad, act_window))
    partners = [(i, i ^ (1 << bit)) for i in range(lax.axis_size(axis))]
    partial = product(mine, kept_grads, kept_acts) + lax.ppermute(sent, axis, partners)
    partial = partial.reshape((len(CHAINS), -1) + partial.shape[1:])
    partial, padded_grad, floats, upward = lax.optimization_barrier(
        (partial, padded_grad, floats, upward)
    )
    inverse = lax.rsqrt(jnp.mean(floats * floats, axis=-1, keepdims=True) + epsilon)
    normed = floats * inverse
    grad_window = jnp.stack(
        [padded_grad[:, taps - 1 - k : taps - 1 - k + length] for k in range(taps)], axis=2
    )
    act_grad = jnp.einsum("blko,kio->bli", grad_window, weight, preferred_element_type=jnp.float32)
    slope_grad = act_grad * gaussian_slope(normed)
    centred = jnp.mean(slope_grad * floats, axis=-1, keepdims=True)
    input_grad = (upward + inverse * slope_grad - floats * inverse**3 * centred).astype(
        jnp.bfloat16
    )
    shared = [step for step in range(len(CHAINS[0])) if len({steps[step] for steps in CHAINS}) == 1]
    for step in range(1, len(CHAINS[0])):
        if step in shared:
            if isinstance(partial, list):
                partial, trunk_input = lax.optimization_barrier((jnp.stack(partial), trunk_input))
            axis, bit = CHAINS[0][step]
            partial = halved(partial, axis, bit, 1 if axis == "seq" else 3)
        else:
            partial = [
                halved(partial[piece], axis, bit, 0 if axis == "seq" else 2)
                for piece, (axis, bit) in enumerate(steps[step] for steps in CHAINS)
            ]
    weight_grad = jnp.transpose(partial.reshape((-1,) + partial.shape[2:]), (1, 2, 0))
    return (trunk_input, input_grad, weight_grad)


def solution(mesh):
    return jax.shard_map(
        shards,
        mesh=mesh,
        in_specs=(P("dp", "seq", None), P(), P("dp", "seq", None)),
        out_specs=(P("dp", None, "seq"), P("dp", "seq", None), P(None, "dp", "seq")),
        check_vma=False,
    )
```

```python
import jax
import jax.numpy as jnp
from jax import lax
from jax.sharding import PartitionSpec as P
import numpy as np

epsilon = 1e-06
root_half = 0.7071067811865476
inv_root_two_pi = 0.3989422804014327


def with_halo(block, sides, width):
    for axis, dim in sides:
        count = lax.axis_size(axis)
        forward = [(i, i + 1) for i in range(count - 1)]
        backward = [(target, source) for source, target in forward]
        low = lax.ppermute(
            lax.slice_in_dim(block, block.shape[dim] - width, None, axis=dim), axis, forward
        )
        high = lax.ppermute(lax.slice_in_dim(block, 0, width, axis=dim), axis, backward)
        block = jnp.concatenate([low, block, high], axis=dim)
    return block


def halved(block, axis, bit, dim):
    count = lax.axis_size(axis)
    partners = [(i, i ^ (1 << bit)) for i in range(count)]
    mine = (lax.axis_index(axis) >> bit) & 1
    half = block.shape[dim] // 2
    keep = lax.dynamic_slice_in_dim(block, mine * half, half, axis=dim)
    send = lax.dynamic_slice_in_dim(block, (1 - mine) * half, half, axis=dim)
    return keep + lax.ppermute(send, axis, partners)


def sources_of(channels, orders):
    pieces = len(orders)
    width = channels // (16 * pieces)
    sources = []
    for piece, bits in enumerate(orders):
        for place in range(16 * width):
            code, rest = divmod(place, width)
            index = 0
            for step, bit in enumerate(bits):
                index |= ((code >> (len(bits) - 1 - step)) & 1) << bit
            sources.append((index * pieces + piece) * width + rest)
    return np.array(sources, np.int32)


def picked(block, sources):
    rows = lax.broadcasted_iota(jnp.int32, (block.shape[-1], sources.shape[0]), 0)
    one_hot = (rows == sources[None, :]).astype(block.dtype)
    moved = jnp.einsum("blc,co->blo", block, one_hot, preferred_element_type=jnp.float32)
    return moved.astype(block.dtype)


CHAINS = (
    (("seq", 0), ("seq", 2), ("seq", 1), ("dp", 0), ("seq", 3), ("dp", 3), ("dp", 1), ("dp", 2)),
    (("seq", 0), ("seq", 1), ("dp", 0), ("seq", 2), ("seq", 3), ("dp", 3), ("dp", 1), ("dp", 2)),
    (("seq", 0), ("dp", 0), ("seq", 2), ("seq", 1), ("seq", 3), ("dp", 3), ("dp", 1), ("dp", 2)),
)


def gaussian_unit(value):
    return 0.5 * value * (1.0 + jax.scipy.special.erf(value * root_half))


def gaussian_slope(value):
    return 0.5 * (
        1.0 + jax.scipy.special.erf(value * root_half)
    ) + value * inv_root_two_pi * jnp.exp(-0.5 * value * value)


def windows(padded, length, taps):
    return jnp.stack([padded[:, offset : offset + length] for offset in range(taps)], axis=2)


def shards(features, weight, cotangent):
    taps = weight.shape[0]
    channels = weight.shape[2]
    batch = features.shape[0]
    length = features.shape[1]
    reach = taps // 2
    floats = features.astype(jnp.float32)
    inverse = lax.rsqrt(jnp.mean(floats * floats, axis=-1, keepdims=True) + epsilon)
    normed = floats * inverse
    activations = gaussian_unit(normed).astype(jnp.bfloat16)
    spread = (
        lax.broadcasted_iota(jnp.int32, (length, length // 2), 0) // 2
        == lax.broadcasted_iota(jnp.int32, (length, length // 2), 1)
    ).astype(cotangent.dtype)
    upward = 0.5 * jnp.einsum("bjc,lj->blc", cotangent, spread, preferred_element_type=jnp.float32)
    branch_grad = upward.astype(jnp.bfloat16)
    count = lax.axis_size("seq")
    forward = [(i, i + 1) for i in range(count - 1)]
    backward = [(target, source) for source, target in forward]
    both = (activations, branch_grad)
    low = lax.ppermute(jnp.concatenate([x[:, length - reach :] for x in both], axis=-1), "seq", forward)
    high = lax.ppermute(jnp.concatenate([x[:, :reach] for x in both], axis=-1), "seq", backward)
    padded_acts, padded_grad = (
        jnp.concatenate([edge_low, x, edge_high], axis=1)
        for x, edge_low, edge_high in zip(
            both, jnp.split(low, 2, axis=-1), jnp.split(high, 2, axis=-1)
        )
    )
    dp_order = tuple(bit for axis, bit in CHAINS[0] if axis == "dp")
    act_window = windows(
        picked(padded_acts, jnp.asarray(sources_of(padded_acts.shape[-1], (dp_order,)))), length, taps
    )
    orders = [tuple(bit for axis, bit in steps if axis == "seq") for steps in CHAINS]
    columns = jnp.asarray(sources_of(channels, orders)).reshape(len(CHAINS), 2, -1)
    axis, bit = CHAINS[0][0]
    mine = (lax.axis_index(axis) >> bit) & 1
    halves = []
    for side in (mine, 1 - mine):
        chosen = lax.dynamic_index_in_dim(columns, side, axis=1, keepdims=False).reshape(-1)
        product = jnp.einsum(
            "blo,blki->oki", picked(branch_grad, chosen), act_window, preferred_element_type=jnp.float32
        )
        halves.append(product)
    partners = [(i, i ^ (1 << bit)) for i in range(lax.axis_size(axis))]
    partial = halves[0] + lax.ppermute(halves[1], axis, partners)
    partial = partial.reshape((len(CHAINS), -1) + partial.shape[1:])
    partial, padded_acts, padded_grad, floats, upward = lax.optimization_barrier(
        (partial, padded_acts, padded_grad, floats, upward)
    )
    inverse = lax.rsqrt(jnp.mean(floats * floats, axis=-1, keepdims=True) + epsilon)
    normed = floats * inverse
    grad_window = jnp.stack(
        [padded_grad[:, taps - 1 - k : taps - 1 - k + length] for k in range(taps)], axis=2
    )
    act_grad = jnp.einsum("blko,kio->bli", grad_window, weight, preferred_element_type=jnp.float32)
    slope_grad = act_grad * gaussian_slope(normed)
    centred = jnp.mean(slope_grad * floats, axis=-1, keepdims=True)
    input_grad = (upward + inverse * slope_grad - floats * inverse**3 * centred).astype(
        jnp.bfloat16
    )
    window = windows(padded_acts, length, taps)
    mixed = jnp.einsum("blki,kio->blo", window, weight, preferred_element_type=jnp.float32)
    summed = floats + mixed
    paired = summed.reshape(batch, length // 2, 2, channels)
    pooled = (0.5 * (paired[:, :, 0] + paired[:, :, 1])).astype(jnp.bfloat16)
    trunk_input = lax.all_to_all(pooled, "seq", split_axis=2, concat_axis=1, tiled=True)
    shared = [step for step in range(len(CHAINS[0])) if len({steps[step] for steps in CHAINS}) == 1]
    for step in range(1, len(CHAINS[0])):
        if step in shared:
            if isinstance(partial, list):
                partial, trunk_input = lax.optimization_barrier((jnp.stack(partial), trunk_input))
            axis, bit = CHAINS[0][step]
            partial = halved(partial, axis, bit, 1 if axis == "seq" else 3)
        else:
            partial = [
                halved(partial[piece], axis, bit, 0 if axis == "seq" else 2)
                for piece, (axis, bit) in enumerate(steps[step] for steps in CHAINS)
            ]
    weight_grad = jnp.transpose(partial.reshape((-1,) + partial.shape[2:]), (1, 2, 0))
    return (trunk_input, input_grad, weight_grad)


def solution(mesh):
    return jax.shard_map(
        shards,
        mesh=mesh,
        in_specs=(P("dp", "seq", None), P(), P("dp", "seq", None)),
        out_specs=(P("dp", None, "seq"), P("dp", "seq", None), P(None, "dp", "seq")),
        check_vma=False,
    )
```

```python
import jax
import jax.numpy as jnp
from jax import lax
from jax.sharding import PartitionSpec as P
import numpy as np

epsilon = 1e-06
root_half = 0.7071067811865476
inv_root_two_pi = 0.3989422804014327


def with_halo(block, sides, width):
    for axis, dim in sides:
        count = lax.axis_size(axis)
        forward = [(i, i + 1) for i in range(count - 1)]
        backward = [(target, source) for source, target in forward]
        low = lax.ppermute(
            lax.slice_in_dim(block, block.shape[dim] - width, None, axis=dim), axis, forward
        )
        high = lax.ppermute(lax.slice_in_dim(block, 0, width, axis=dim), axis, backward)
        block = jnp.concatenate([low, block, high], axis=dim)
    return block


def halved(block, axis, bit, dim):
    count = lax.axis_size(axis)
    partners = [(i, i ^ (1 << bit)) for i in range(count)]
    mine = (lax.axis_index(axis) >> bit) & 1
    half = block.shape[dim] // 2
    keep = lax.dynamic_slice_in_dim(block, mine * half, half, axis=dim)
    send = lax.dynamic_slice_in_dim(block, (1 - mine) * half, half, axis=dim)
    return keep + lax.ppermute(send, axis, partners)


def sources_of(channels, orders):
    pieces = len(orders)
    width = channels // (16 * pieces)
    sources = []
    for piece, bits in enumerate(orders):
        for place in range(16 * width):
            code, rest = divmod(place, width)
            index = 0
            for step, bit in enumerate(bits):
                index |= ((code >> (len(bits) - 1 - step)) & 1) << bit
            sources.append((index * pieces + piece) * width + rest)
    return np.array(sources, np.int32)


def picked(block, sources):
    rows = lax.broadcasted_iota(jnp.int32, (block.shape[-1], sources.shape[0]), 0)
    one_hot = (rows == sources[None, :]).astype(block.dtype)
    moved = jnp.einsum("blc,co->blo", block, one_hot, preferred_element_type=jnp.float32)
    return moved.astype(block.dtype)


CHAINS = (
    (("seq", 0), ("seq", 2), ("seq", 1), ("dp", 0), ("seq", 3), ("dp", 3), ("dp", 1), ("dp", 2)),
    (("seq", 0), ("seq", 1), ("dp", 0), ("seq", 2), ("seq", 3), ("dp", 3), ("dp", 1), ("dp", 2)),
    (("seq", 0), ("dp", 0), ("seq", 2), ("seq", 1), ("seq", 3), ("dp", 3), ("dp", 1), ("dp", 2)),
)


def gaussian_unit(value):
    return 0.5 * value * (1.0 + jax.scipy.special.erf(value * root_half))


def gaussian_slope(value):
    return 0.5 * (
        1.0 + jax.scipy.special.erf(value * root_half)
    ) + value * inv_root_two_pi * jnp.exp(-0.5 * value * value)


def windows(padded, length, taps):
    return jnp.stack([padded[:, offset : offset + length] for offset in range(taps)], axis=2)


def shards(features, weight, cotangent):
    taps = weight.shape[0]
    channels = weight.shape[2]
    batch = features.shape[0]
    length = features.shape[1]
    reach = taps // 2
    floats = features.astype(jnp.float32)
    inverse = lax.rsqrt(jnp.mean(floats * floats, axis=-1, keepdims=True) + epsilon)
    normed = floats * inverse
    activations = gaussian_unit(normed).astype(jnp.bfloat16)
    spread = (
        lax.broadcasted_iota(jnp.int32, (length, length // 2), 0) // 2
        == lax.broadcasted_iota(jnp.int32, (length, length // 2), 1)
    ).astype(cotangent.dtype)
    upward = 0.5 * jnp.einsum("bjc,lj->blc", cotangent, spread, preferred_element_type=jnp.float32)
    branch_grad = upward.astype(jnp.bfloat16)
    padded_acts = with_halo(activations, (("seq", 1),), reach)
    padded_grad = with_halo(branch_grad, (("seq", 1),), reach)
    dp_order = tuple(bit for axis, bit in CHAINS[0] if axis == "dp")
    act_window = windows(
        picked(padded_acts, jnp.asarray(sources_of(padded_acts.shape[-1], (dp_order,)))), length, taps
    )
    orders = [tuple(bit for axis, bit in steps if axis == "seq") for steps in CHAINS]
    columns = jnp.asarray(sources_of(channels, orders)).reshape(len(CHAINS), 2, -1)
    axis, bit = CHAINS[0][0]
    mine = (lax.axis_index(axis) >> bit) & 1
    halves = []
    for side in (mine, 1 - mine):
        chosen = lax.dynamic_index_in_dim(columns, side, axis=1, keepdims=False).reshape(-1)
        product = jnp.einsum(
            "blo,blki->oki", picked(branch_grad, chosen), act_window, preferred_element_type=jnp.float32
        )
        halves.append(product)
    partners = [(i, i ^ (1 << bit)) for i in range(lax.axis_size(axis))]
    partial = halves[0] + lax.ppermute(halves[1], axis, partners)
    partial = partial.reshape((len(CHAINS), -1) + partial.shape[1:])
    partial, padded_acts, padded_grad, floats, upward = lax.optimization_barrier(
        (partial, padded_acts, padded_grad, floats, upward)
    )
    inverse = lax.rsqrt(jnp.mean(floats * floats, axis=-1, keepdims=True) + epsilon)
    normed = floats * inverse
    grad_window = jnp.stack(
        [padded_grad[:, taps - 1 - k : taps - 1 - k + length] for k in range(taps)], axis=2
    )
    act_grad = jnp.einsum("blko,kio->bli", grad_window, weight, preferred_element_type=jnp.float32)
    slope_grad = act_grad * gaussian_slope(normed)
    centred = jnp.mean(slope_grad * floats, axis=-1, keepdims=True)
    input_grad = (upward + inverse * slope_grad - floats * inverse**3 * centred).astype(
        jnp.bfloat16
    )
    summed = [
        floats[:, parity::2]
        + jnp.einsum(
            "blki,kio->blo",
            jnp.stack(
                [padded_acts[:, parity + k : parity + k + length : 2] for k in range(taps)], axis=2
            ),
            weight,
            preferred_element_type=jnp.float32,
        )
        for parity in (0, 1)
    ]
    pooled = (0.5 * (summed[0] + summed[1])).astype(jnp.bfloat16)
    trunk_input = lax.all_to_all(pooled, "seq", split_axis=2, concat_axis=1, tiled=True)
    shared = [step for step in range(len(CHAINS[0])) if len({steps[step] for steps in CHAINS}) == 1]
    for step in range(1, len(CHAINS[0])):
        if step in shared:
            if isinstance(partial, list):
                partial, trunk_input = lax.optimization_barrier((jnp.stack(partial), trunk_input))
            axis, bit = CHAINS[0][step]
            partial = halved(partial, axis, bit, 1 if axis == "seq" else 3)
        else:
            partial = [
                halved(partial[piece], axis, bit, 0 if axis == "seq" else 2)
                for piece, (axis, bit) in enumerate(steps[step] for steps in CHAINS)
            ]
    weight_grad = jnp.transpose(partial.reshape((-1,) + partial.shape[2:]), (1, 2, 0))
    return (trunk_input, input_grad, weight_grad)


def solution(mesh):
    return jax.shard_map(
        shards,
        mesh=mesh,
        in_specs=(P("dp", "seq", None), P(), P("dp", "seq", None)),
        out_specs=(P("dp", None, "seq"), P("dp", "seq", None), P(None, "dp", "seq")),
        check_vma=False,
    )
```

```python
import jax
import jax.numpy as jnp
from jax import lax
from jax.sharding import PartitionSpec as P
import numpy as np

epsilon = 1e-06
root_half = 0.7071067811865476
inv_root_two_pi = 0.3989422804014327


def with_halo(block, sides, width):
    for axis, dim in sides:
        count = lax.axis_size(axis)
        forward = [(i, i + 1) for i in range(count - 1)]
        backward = [(target, source) for source, target in forward]
        low = lax.ppermute(
            lax.slice_in_dim(block, block.shape[dim] - width, None, axis=dim), axis, forward
        )
        high = lax.ppermute(lax.slice_in_dim(block, 0, width, axis=dim), axis, backward)
        block = jnp.concatenate([low, block, high], axis=dim)
    return block


def halved(block, axis, bit, dim):
    count = lax.axis_size(axis)
    partners = [(i, i ^ (1 << bit)) for i in range(count)]
    mine = (lax.axis_index(axis) >> bit) & 1
    half = block.shape[dim] // 2
    keep = lax.dynamic_slice_in_dim(block, mine * half, half, axis=dim)
    send = lax.dynamic_slice_in_dim(block, (1 - mine) * half, half, axis=dim)
    return keep + lax.ppermute(send, axis, partners)


def sources_of(channels, orders):
    pieces = len(orders)
    width = channels // (16 * pieces)
    sources = []
    for piece, bits in enumerate(orders):
        for place in range(16 * width):
            code, rest = divmod(place, width)
            index = 0
            for step, bit in enumerate(bits):
                index |= ((code >> (len(bits) - 1 - step)) & 1) << bit
            sources.append((index * pieces + piece) * width + rest)
    return np.array(sources, np.int32)


def picked(block, sources):
    rows = lax.broadcasted_iota(jnp.int32, (block.shape[-1], sources.shape[0]), 0)
    one_hot = (rows == sources[None, :]).astype(block.dtype)
    moved = jnp.einsum("blc,co->blo", block, one_hot, preferred_element_type=jnp.float32)
    return moved.astype(block.dtype)


CHAINS = (
    (("seq", 0), ("seq", 2), ("seq", 1), ("dp", 0), ("dp", 2), ("seq", 3), ("dp", 3), ("dp", 1)),
    (("seq", 0), ("seq", 1), ("dp", 0), ("seq", 2), ("dp", 2), ("seq", 3), ("dp", 3), ("dp", 1)),
    (("seq", 0), ("dp", 0), ("seq", 2), ("seq", 1), ("dp", 2), ("seq", 3), ("dp", 3), ("dp", 1)),
)


def gaussian_unit(value):
    return 0.5 * value * (1.0 + jax.scipy.special.erf(value * root_half))


def gaussian_slope(value):
    return 0.5 * (
        1.0 + jax.scipy.special.erf(value * root_half)
    ) + value * inv_root_two_pi * jnp.exp(-0.5 * value * value)


def windows(padded, length, taps):
    return jnp.stack([padded[:, offset : offset + length] for offset in range(taps)], axis=2)


def shards(features, weight, cotangent):
    taps = weight.shape[0]
    channels = weight.shape[2]
    batch = features.shape[0]
    length = features.shape[1]
    reach = taps // 2
    floats = features.astype(jnp.float32)
    inverse = lax.rsqrt(jnp.mean(floats * floats, axis=-1, keepdims=True) + epsilon)
    normed = floats * inverse
    activations = gaussian_unit(normed).astype(jnp.bfloat16)
    spread = (
        lax.broadcasted_iota(jnp.int32, (length, length // 2), 0) // 2
        == lax.broadcasted_iota(jnp.int32, (length, length // 2), 1)
    ).astype(cotangent.dtype)
    upward = 0.5 * jnp.einsum("bjc,lj->blc", cotangent, spread, preferred_element_type=jnp.float32)
    branch_grad = upward.astype(jnp.bfloat16)
    padded_acts = with_halo(activations, (("seq", 1),), reach)
    padded_grad = with_halo(branch_grad, (("seq", 1),), reach)
    dp_order = tuple(bit for axis, bit in CHAINS[0] if axis == "dp")
    act_window = windows(
        picked(padded_acts, jnp.asarray(sources_of(padded_acts.shape[-1], (dp_order,)))), length, taps
    )
    orders = [tuple(bit for axis, bit in steps if axis == "seq") for steps in CHAINS]
    columns = jnp.asarray(sources_of(channels, orders)).reshape(len(CHAINS), 2, -1)
    axis, bit = CHAINS[0][0]
    mine = (lax.axis_index(axis) >> bit) & 1
    halves = []
    for side in (mine, 1 - mine):
        chosen = lax.dynamic_index_in_dim(columns, side, axis=1, keepdims=False).reshape(-1)
        product = jnp.einsum(
            "blo,blki->oki", picked(branch_grad, chosen), act_window, preferred_element_type=jnp.float32
        )
        halves.append(product)
    partners = [(i, i ^ (1 << bit)) for i in range(lax.axis_size(axis))]
    partial = halves[0] + lax.ppermute(halves[1], axis, partners)
    partial = partial.reshape((len(CHAINS), -1) + partial.shape[1:])
    partial, padded_acts, padded_grad, floats, upward = lax.optimization_barrier(
        (partial, padded_acts, padded_grad, floats, upward)
    )
    inverse = lax.rsqrt(jnp.mean(floats * floats, axis=-1, keepdims=True) + epsilon)
    normed = floats * inverse
    grad_window = jnp.stack(
        [padded_grad[:, taps - 1 - k : taps - 1 - k + length] for k in range(taps)], axis=2
    )
    act_grad = jnp.einsum("blko,kio->bli", grad_window, weight, preferred_element_type=jnp.float32)
    slope_grad = act_grad * gaussian_slope(normed)
    centred = jnp.mean(slope_grad * floats, axis=-1, keepdims=True)
    input_grad = (upward + inverse * slope_grad - floats * inverse**3 * centred).astype(
        jnp.bfloat16
    )
    window = windows(padded_acts, length, taps)
    mixed = jnp.einsum("blki,kio->blo", window, weight, preferred_element_type=jnp.float32)
    summed = floats + mixed
    paired = summed.reshape(batch, length // 2, 2, channels)
    pooled = (0.5 * (paired[:, :, 0] + paired[:, :, 1])).astype(jnp.bfloat16)
    trunk_input = lax.all_to_all(pooled, "seq", split_axis=2, concat_axis=1, tiled=True)
    shared = [step for step in range(len(CHAINS[0])) if len({steps[step] for steps in CHAINS}) == 1]
    for step in range(1, len(CHAINS[0])):
        if step in shared:
            if isinstance(partial, list):
                partial, trunk_input = lax.optimization_barrier((jnp.stack(partial), trunk_input))
            axis, bit = CHAINS[0][step]
            partial = halved(partial, axis, bit, 1 if axis == "seq" else 3)
        else:
            partial = [
                halved(partial[piece], axis, bit, 0 if axis == "seq" else 2)
                for piece, (axis, bit) in enumerate(steps[step] for steps in CHAINS)
            ]
    weight_grad = jnp.transpose(partial.reshape((-1,) + partial.shape[2:]), (1, 2, 0))
    return (trunk_input, input_grad, weight_grad)


def solution(mesh):
    return jax.shard_map(
        shards,
        mesh=mesh,
        in_specs=(P("dp", "seq", None), P(), P("dp", "seq", None)),
        out_specs=(P("dp", None, "seq"), P("dp", "seq", None), P(None, "dp", "seq")),
        check_vma=False,
    )
```

```python
import jax
import jax.numpy as jnp
from jax import lax
from jax.sharding import PartitionSpec as P
import numpy as np

epsilon = 1e-06
root_half = 0.7071067811865476
inv_root_two_pi = 0.3989422804014327


def with_halo(block, sides, width):
    for axis, dim in sides:
        count = lax.axis_size(axis)
        forward = [(i, i + 1) for i in range(count - 1)]
        backward = [(target, source) for source, target in forward]
        low = lax.ppermute(
            lax.slice_in_dim(block, block.shape[dim] - width, None, axis=dim), axis, forward
        )
        high = lax.ppermute(lax.slice_in_dim(block, 0, width, axis=dim), axis, backward)
        block = jnp.concatenate([low, block, high], axis=dim)
    return block


def halved(block, axis, bit, dim):
    count = lax.axis_size(axis)
    partners = [(i, i ^ (1 << bit)) for i in range(count)]
    mine = (lax.axis_index(axis) >> bit) & 1
    half = block.shape[dim] // 2
    keep = lax.dynamic_slice_in_dim(block, mine * half, half, axis=dim)
    send = lax.dynamic_slice_in_dim(block, (1 - mine) * half, half, axis=dim)
    return keep + lax.ppermute(send, axis, partners)


def sources_of(channels, orders):
    pieces = len(orders)
    width = channels // (16 * pieces)
    sources = []
    for piece, bits in enumerate(orders):
        for place in range(16 * width):
            code, rest = divmod(place, width)
            index = 0
            for step, bit in enumerate(bits):
                index |= ((code >> (len(bits) - 1 - step)) & 1) << bit
            sources.append((index * pieces + piece) * width + rest)
    return np.array(sources, np.int32)


def picked(block, sources):
    rows = lax.broadcasted_iota(jnp.int32, (block.shape[-1], sources.shape[0]), 0)
    one_hot = (rows == sources[None, :]).astype(block.dtype)
    moved = jnp.einsum("blc,co->blo", block, one_hot, preferred_element_type=jnp.float32)
    return moved.astype(block.dtype)


CHAINS = (
    (("seq", 0), ("seq", 2), ("seq", 1), ("dp", 0), ("seq", 3), ("dp", 3), ("dp", 1), ("dp", 2)),
    (("seq", 0), ("seq", 1), ("dp", 0), ("seq", 2), ("seq", 3), ("dp", 3), ("dp", 1), ("dp", 2)),
    (("seq", 0), ("dp", 0), ("seq", 2), ("seq", 1), ("seq", 3), ("dp", 3), ("dp", 1), ("dp", 2)),
)


def gaussian_unit(value):
    return 0.5 * value * (1.0 + jax.scipy.special.erf(value * root_half))


def gaussian_slope(value):
    return 0.5 * (
        1.0 + jax.scipy.special.erf(value * root_half)
    ) + value * inv_root_two_pi * jnp.exp(-0.5 * value * value)


def windows(padded, length, taps):
    return jnp.stack([padded[:, offset : offset + length] for offset in range(taps)], axis=2)


def shards(features, weight, cotangent):
    taps = weight.shape[0]
    channels = weight.shape[2]
    batch = features.shape[0]
    length = features.shape[1]
    reach = taps // 2
    floats = features.astype(jnp.float32)
    inverse = lax.rsqrt(jnp.mean(floats * floats, axis=-1, keepdims=True) + epsilon)
    normed = floats * inverse
    activations = gaussian_unit(normed).astype(jnp.bfloat16)
    spread = (
        lax.broadcasted_iota(jnp.int32, (length, length // 2), 0) // 2
        == lax.broadcasted_iota(jnp.int32, (length, length // 2), 1)
    ).astype(cotangent.dtype)
    upward = 0.5 * jnp.einsum("bjc,lj->blc", cotangent, spread, preferred_element_type=jnp.float32)
    branch_grad = upward.astype(jnp.bfloat16)
    padded_acts = with_halo(activations, (("seq", 1),), reach)
    padded_grad = with_halo(branch_grad, (("seq", 1),), reach)
    dp_order = tuple(bit for axis, bit in CHAINS[0] if axis == "dp")
    act_window = windows(
        picked(padded_acts, jnp.asarray(sources_of(padded_acts.shape[-1], (dp_order,)))), length, taps
    )
    orders = [tuple(bit for axis, bit in steps if axis == "seq") for steps in CHAINS]
    columns = jnp.asarray(sources_of(channels, orders)).reshape(len(CHAINS), 2, -1)
    axis, bit = CHAINS[0][0]
    mine = (lax.axis_index(axis) >> bit) & 1
    halves = []
    for side in (mine, 1 - mine):
        chosen = lax.dynamic_index_in_dim(columns, side, axis=1, keepdims=False).reshape(-1)
        product = jnp.einsum(
            "blo,blki->oki", picked(branch_grad, chosen), act_window, preferred_element_type=jnp.float32
        )
        halves.append(product)
    partners = [(i, i ^ (1 << bit)) for i in range(lax.axis_size(axis))]
    partial = halves[0] + lax.ppermute(halves[1], axis, partners)
    partial = partial.reshape((len(CHAINS), -1) + partial.shape[1:])
    partial, padded_acts, padded_grad, floats, upward = lax.optimization_barrier(
        (partial, padded_acts, padded_grad, floats, upward)
    )
    inverse = lax.rsqrt(jnp.mean(floats * floats, axis=-1, keepdims=True) + epsilon)
    normed = floats * inverse
    grad_window = jnp.stack(
        [padded_grad[:, taps - 1 - k : taps - 1 - k + length] for k in range(taps)], axis=2
    )
    act_grad = jnp.einsum("blko,kio->bli", grad_window, weight, preferred_element_type=jnp.float32)
    slope_grad = act_grad * gaussian_slope(normed)
    centred = jnp.mean(slope_grad * floats, axis=-1, keepdims=True)
    input_grad = (upward + inverse * slope_grad - floats * inverse**3 * centred).astype(
        jnp.bfloat16
    )
    window = windows(padded_acts, length, taps)
    mixed = jnp.einsum("blki,kio->blo", window, weight, preferred_element_type=jnp.float32)
    summed = floats + mixed
    paired = summed.reshape(batch, length // 2, 2, channels)
    pooled = (0.5 * (paired[:, :, 0] + paired[:, :, 1])).astype(jnp.bfloat16)
    trunk_input = lax.all_to_all(pooled, "seq", split_axis=2, concat_axis=1, tiled=True)
    shared = [step for step in range(len(CHAINS[0])) if len({steps[step] for steps in CHAINS}) == 1]
    for step in range(1, len(CHAINS[0])):
        if step in shared:
            joining = isinstance(partial, list)
            if joining:
                partial = jnp.stack(partial)
            axis, bit = CHAINS[0][step]
            partial = halved(partial, axis, bit, 1 if axis == "seq" else 3)
            if joining:
                partial, trunk_input = lax.optimization_barrier((partial, trunk_input))
        else:
            partial = [
                halved(partial[piece], axis, bit, 0 if axis == "seq" else 2)
                for piece, (axis, bit) in enumerate(steps[step] for steps in CHAINS)
            ]
    weight_grad = jnp.transpose(partial.reshape((-1,) + partial.shape[2:]), (1, 2, 0))
    return (trunk_input, input_grad, weight_grad)


def solution(mesh):
    return jax.shard_map(
        shards,
        mesh=mesh,
        in_specs=(P("dp", "seq", None), P(), P("dp", "seq", None)),
        out_specs=(P("dp", None, "seq"), P("dp", "seq", None), P(None, "dp", "seq")),
        check_vma=False,
    )
```

```python
import jax
import jax.numpy as jnp
from jax import lax
from jax.sharding import PartitionSpec as P
import numpy as np

epsilon = 1e-06
root_half = 0.7071067811865476
inv_root_two_pi = 0.3989422804014327


def with_halo(block, sides, width):
    for axis, dim in sides:
        count = lax.axis_size(axis)
        forward = [(i, i + 1) for i in range(count - 1)]
        backward = [(target, source) for source, target in forward]
        low = lax.ppermute(
            lax.slice_in_dim(block, block.shape[dim] - width, None, axis=dim), axis, forward
        )
        high = lax.ppermute(lax.slice_in_dim(block, 0, width, axis=dim), axis, backward)
        block = jnp.concatenate([low, block, high], axis=dim)
    return block


def halved(block, axis, bit, dim):
    count = lax.axis_size(axis)
    partners = [(i, i ^ (1 << bit)) for i in range(count)]
    mine = (lax.axis_index(axis) >> bit) & 1
    half = block.shape[dim] // 2
    keep = lax.dynamic_slice_in_dim(block, mine * half, half, axis=dim)
    send = lax.dynamic_slice_in_dim(block, (1 - mine) * half, half, axis=dim)
    return keep + lax.ppermute(send, axis, partners)


def sources_of(channels, orders):
    pieces = len(orders)
    width = channels // (16 * pieces)
    sources = []
    for piece, bits in enumerate(orders):
        for place in range(16 * width):
            code, rest = divmod(place, width)
            index = 0
            for step, bit in enumerate(bits):
                index |= ((code >> (len(bits) - 1 - step)) & 1) << bit
            sources.append((index * pieces + piece) * width + rest)
    return np.array(sources, np.int32)


def picked(block, sources):
    rows = lax.broadcasted_iota(jnp.int32, (block.shape[-1], sources.shape[0]), 0)
    one_hot = (rows == sources[None, :]).astype(block.dtype)
    moved = jnp.einsum("blc,co->blo", block, one_hot, preferred_element_type=jnp.float32)
    return moved.astype(block.dtype)


CHAINS = (
    (("seq", 0), ("seq", 2), ("seq", 1), ("dp", 0), ("seq", 3), ("dp", 3), ("dp", 1), ("dp", 2)),
    (("seq", 0), ("seq", 1), ("dp", 0), ("seq", 2), ("seq", 3), ("dp", 3), ("dp", 1), ("dp", 2)),
    (("seq", 0), ("dp", 0), ("seq", 2), ("seq", 1), ("seq", 3), ("dp", 3), ("dp", 1), ("dp", 2)),
)


def gaussian_unit(value):
    return 0.5 * value * (1.0 + jax.scipy.special.erf(value * root_half))


def gaussian_slope(value):
    return 0.5 * (
        1.0 + jax.scipy.special.erf(value * root_half)
    ) + value * inv_root_two_pi * jnp.exp(-0.5 * value * value)


def windows(padded, length, taps):
    return jnp.stack([padded[:, offset : offset + length] for offset in range(taps)], axis=2)


def shards(features, weight, cotangent):
    taps = weight.shape[0]
    channels = weight.shape[2]
    batch = features.shape[0]
    length = features.shape[1]
    reach = taps // 2
    floats = features.astype(jnp.float32)
    inverse = lax.rsqrt(jnp.mean(floats * floats, axis=-1, keepdims=True) + epsilon)
    normed = floats * inverse
    activations = gaussian_unit(normed).astype(jnp.bfloat16)
    spread = (
        lax.broadcasted_iota(jnp.int32, (length, length // 2), 0) // 2
        == lax.broadcasted_iota(jnp.int32, (length, length // 2), 1)
    ).astype(cotangent.dtype)
    upward = 0.5 * jnp.einsum("bjc,lj->blc", cotangent, spread, preferred_element_type=jnp.float32)
    branch_grad = upward.astype(jnp.bfloat16)
    padded_acts = with_halo(activations, (("seq", 1),), reach)
    padded_grad = with_halo(branch_grad, (("seq", 1),), reach)
    dp_order = tuple(bit for axis, bit in CHAINS[0] if axis == "dp")
    act_window = windows(
        picked(padded_acts, jnp.asarray(sources_of(padded_acts.shape[-1], (dp_order,)))), length, taps
    )
    orders = [tuple(bit for axis, bit in steps if axis == "seq") for steps in CHAINS]
    columns = jnp.asarray(sources_of(channels, orders)).reshape(len(CHAINS), 2, -1)
    axis, bit = CHAINS[0][0]
    mine = (lax.axis_index(axis) >> bit) & 1
    halves = []
    for side in (mine, 1 - mine):
        chosen = lax.dynamic_index_in_dim(columns, side, axis=1, keepdims=False).reshape(-1)
        product = jnp.einsum(
            "blo,blki->oki", picked(branch_grad, chosen), act_window, preferred_element_type=jnp.float32
        )
        halves.append(product)
    partners = [(i, i ^ (1 << bit)) for i in range(lax.axis_size(axis))]
    partial = halves[0] + lax.ppermute(halves[1], axis, partners)
    partial = partial.reshape((len(CHAINS), -1) + partial.shape[1:])
    partial, padded_acts, padded_grad, floats, upward = lax.optimization_barrier(
        (partial, padded_acts, padded_grad, floats, upward)
    )
    inverse = lax.rsqrt(jnp.mean(floats * floats, axis=-1, keepdims=True) + epsilon)
    normed = floats * inverse
    grad_window = jnp.stack(
        [padded_grad[:, taps - 1 - k : taps - 1 - k + length] for k in range(taps)], axis=2
    )
    act_grad = jnp.einsum("blko,kio->bli", grad_window, weight, preferred_element_type=jnp.float32)
    slope_grad = act_grad * gaussian_slope(normed)
    centred = jnp.mean(slope_grad * floats, axis=-1, keepdims=True)
    input_grad = (upward + inverse * slope_grad - floats * inverse**3 * centred).astype(
        jnp.bfloat16
    )
    window = windows(padded_acts, length, taps)
    mixed = jnp.einsum("blki,kio->blo", window, weight, preferred_element_type=jnp.float32)
    summed = floats + mixed
    paired = summed.reshape(batch, length // 2, 2, channels)
    pooled = (0.5 * (paired[:, :, 0] + paired[:, :, 1])).astype(jnp.bfloat16)
    trunk_input = lax.all_to_all(pooled, "seq", split_axis=2, concat_axis=1, tiled=True)
    shared = [step for step in range(len(CHAINS[0])) if len({steps[step] for steps in CHAINS}) == 1]
    for step in range(1, len(CHAINS[0])):
        if step in shared:
            if isinstance(partial, list):
                partial = jnp.stack(partial)
            axis, bit = CHAINS[0][step]
            partial = halved(partial, axis, bit, 1 if axis == "seq" else 3)
            if step == shared[2]:
                partial, trunk_input = lax.optimization_barrier((partial, trunk_input))
        else:
            partial = [
                halved(partial[piece], axis, bit, 0 if axis == "seq" else 2)
                for piece, (axis, bit) in enumerate(steps[step] for steps in CHAINS)
            ]
    weight_grad = jnp.transpose(partial.reshape((-1,) + partial.shape[2:]), (1, 2, 0))
    return (trunk_input, input_grad, weight_grad)


def solution(mesh):
    return jax.shard_map(
        shards,
        mesh=mesh,
        in_specs=(P("dp", "seq", None), P(), P("dp", "seq", None)),
        out_specs=(P("dp", None, "seq"), P("dp", "seq", None), P(None, "dp", "seq")),
        check_vma=False,
    )
```

```python
import jax
import jax.numpy as jnp
from jax import lax
from jax.sharding import PartitionSpec as P
import numpy as np

epsilon = 1e-06
root_half = 0.7071067811865476
inv_root_two_pi = 0.3989422804014327


def with_halo(block, sides, width):
    for axis, dim in sides:
        count = lax.axis_size(axis)
        forward = [(i, i + 1) for i in range(count - 1)]
        backward = [(target, source) for source, target in forward]
        low = lax.ppermute(
            lax.slice_in_dim(block, block.shape[dim] - width, None, axis=dim), axis, forward
        )
        high = lax.ppermute(lax.slice_in_dim(block, 0, width, axis=dim), axis, backward)
        block = jnp.concatenate([low, block, high], axis=dim)
    return block


def halved(block, axis, bit, dim):
    count = lax.axis_size(axis)
    partners = [(i, i ^ (1 << bit)) for i in range(count)]
    mine = (lax.axis_index(axis) >> bit) & 1
    half = block.shape[dim] // 2
    keep = lax.dynamic_slice_in_dim(block, mine * half, half, axis=dim)
    send = lax.dynamic_slice_in_dim(block, (1 - mine) * half, half, axis=dim)
    return keep + lax.ppermute(send, axis, partners)


def sources_of(channels, orders):
    pieces = len(orders)
    width = channels // (16 * pieces)
    sources = []
    for piece, bits in enumerate(orders):
        for place in range(16 * width):
            code, rest = divmod(place, width)
            index = 0
            for step, bit in enumerate(bits):
                index |= ((code >> (len(bits) - 1 - step)) & 1) << bit
            sources.append((index * pieces + piece) * width + rest)
    return np.array(sources, np.int32)


def picked(block, sources):
    rows = lax.broadcasted_iota(jnp.int32, (block.shape[-1], sources.shape[0]), 0)
    one_hot = (rows == sources[None, :]).astype(block.dtype)
    moved = jnp.einsum("blc,co->blo", block, one_hot, preferred_element_type=jnp.float32)
    return moved.astype(block.dtype)


CHAINS = (
    (("seq", 0), ("seq", 2), ("seq", 1), ("dp", 0), ("seq", 3), ("dp", 3), ("dp", 1), ("dp", 2)),
    (("seq", 0), ("seq", 1), ("dp", 0), ("seq", 2), ("seq", 3), ("dp", 3), ("dp", 1), ("dp", 2)),
    (("seq", 0), ("dp", 0), ("seq", 2), ("seq", 1), ("seq", 3), ("dp", 3), ("dp", 1), ("dp", 2)),
)


def gaussian_unit(value):
    return 0.5 * value * (1.0 + jax.scipy.special.erf(value * root_half))


def gaussian_slope(value):
    return 0.5 * (
        1.0 + jax.scipy.special.erf(value * root_half)
    ) + value * inv_root_two_pi * jnp.exp(-0.5 * value * value)


def windows(padded, length, taps):
    return jnp.stack([padded[:, offset : offset + length] for offset in range(taps)], axis=2)


def shards(features, weight, cotangent):
    taps = weight.shape[0]
    channels = weight.shape[2]
    batch = features.shape[0]
    length = features.shape[1]
    reach = taps // 2
    floats = features.astype(jnp.float32)
    inverse = lax.rsqrt(jnp.mean(floats * floats, axis=-1, keepdims=True) + epsilon)
    normed = floats * inverse
    activations = gaussian_unit(normed).astype(jnp.bfloat16)
    spread = (
        lax.broadcasted_iota(jnp.int32, (length, length // 2), 0) // 2
        == lax.broadcasted_iota(jnp.int32, (length, length // 2), 1)
    ).astype(cotangent.dtype)
    upward = 0.5 * jnp.einsum("bjc,lj->blc", cotangent, spread, preferred_element_type=jnp.float32)
    branch_grad = upward.astype(jnp.bfloat16)
    padded_acts = with_halo(activations, (("seq", 1),), reach)
    padded_grad = with_halo(branch_grad, (("seq", 1),), reach)
    dp_order = tuple(bit for axis, bit in CHAINS[0] if axis == "dp")
    act_window = windows(
        picked(padded_acts, jnp.asarray(sources_of(padded_acts.shape[-1], (dp_order,)))), length, taps
    )
    orders = [tuple(bit for axis, bit in steps if axis == "seq") for steps in CHAINS]
    columns = jnp.asarray(sources_of(channels, orders)).reshape(len(CHAINS), 2, -1)
    axis, bit = CHAINS[0][0]
    mine = (lax.axis_index(axis) >> bit) & 1
    halves = []
    for side in (mine, 1 - mine):
        chosen = lax.dynamic_index_in_dim(columns, side, axis=1, keepdims=False).reshape(-1)
        product = jnp.einsum(
            "blo,blki->oki", picked(branch_grad, chosen), act_window, preferred_element_type=jnp.float32
        )
        halves.append(product)
    partners = [(i, i ^ (1 << bit)) for i in range(lax.axis_size(axis))]
    partial = halves[0] + lax.ppermute(halves[1], axis, partners)
    partial = partial.reshape((len(CHAINS), -1) + partial.shape[1:])
    partial, padded_acts, padded_grad, floats, upward = lax.optimization_barrier(
        (partial, padded_acts, padded_grad, floats, upward)
    )
    inverse = lax.rsqrt(jnp.mean(floats * floats, axis=-1, keepdims=True) + epsilon)
    normed = floats * inverse
    grad_window = jnp.stack(
        [padded_grad[:, taps - 1 - k : taps - 1 - k + length] for k in range(taps)], axis=2
    )
    act_grad = jnp.einsum("blko,kio->bli", grad_window, weight, preferred_element_type=jnp.float32)
    slope_grad = act_grad * gaussian_slope(normed)
    centred = jnp.mean(slope_grad * floats, axis=-1, keepdims=True)
    input_grad = (upward + inverse * slope_grad - floats * inverse**3 * centred).astype(
        jnp.bfloat16
    )
    window = windows(padded_acts, length, taps)
    mixed = jnp.einsum("blki,kio->blo", window, weight, preferred_element_type=jnp.float32)
    summed = floats + mixed
    paired = summed.reshape(batch, length // 2, 2, channels)
    pooled = (0.5 * (paired[:, :, 0] + paired[:, :, 1])).astype(jnp.bfloat16)
    trunk_input = lax.all_to_all(pooled, "seq", split_axis=2, concat_axis=1, tiled=True)
    shared = [step for step in range(len(CHAINS[0])) if len({steps[step] for steps in CHAINS}) == 1]
    for step in range(1, len(CHAINS[0])):
        if step in shared:
            if isinstance(partial, list):
                partial = jnp.stack(partial)
            axis, bit = CHAINS[0][step]
            partial = halved(partial, axis, bit, 1 if axis == "seq" else 3)
            if step == shared[3]:
                partial, trunk_input = lax.optimization_barrier((partial, trunk_input))
        else:
            partial = [
                halved(partial[piece], axis, bit, 0 if axis == "seq" else 2)
                for piece, (axis, bit) in enumerate(steps[step] for steps in CHAINS)
            ]
    weight_grad = jnp.transpose(partial.reshape((-1,) + partial.shape[2:]), (1, 2, 0))
    return (trunk_input, input_grad, weight_grad)


def solution(mesh):
    return jax.shard_map(
        shards,
        mesh=mesh,
        in_specs=(P("dp", "seq", None), P(), P("dp", "seq", None)),
        out_specs=(P("dp", None, "seq"), P("dp", "seq", None), P(None, "dp", "seq")),
        check_vma=False,
    )
```

```python
import jax
import jax.numpy as jnp
from jax import lax
from jax.sharding import PartitionSpec as P
import numpy as np

epsilon = 1e-06
root_half = 0.7071067811865476
inv_root_two_pi = 0.3989422804014327


def with_halo(block, sides, width):
    for axis, dim in sides:
        count = lax.axis_size(axis)
        forward = [(i, i + 1) for i in range(count - 1)]
        backward = [(target, source) for source, target in forward]
        low = lax.ppermute(
            lax.slice_in_dim(block, block.shape[dim] - width, None, axis=dim), axis, forward
        )
        high = lax.ppermute(lax.slice_in_dim(block, 0, width, axis=dim), axis, backward)
        block = jnp.concatenate([low, block, high], axis=dim)
    return block


def halved(block, axis, bit, dim):
    count = lax.axis_size(axis)
    partners = [(i, i ^ (1 << bit)) for i in range(count)]
    mine = (lax.axis_index(axis) >> bit) & 1
    half = block.shape[dim] // 2
    keep = lax.dynamic_slice_in_dim(block, mine * half, half, axis=dim)
    send = lax.dynamic_slice_in_dim(block, (1 - mine) * half, half, axis=dim)
    return keep + lax.ppermute(send, axis, partners)


def sources_of(channels, orders):
    pieces = len(orders)
    width = channels // (16 * pieces)
    sources = []
    for piece, bits in enumerate(orders):
        for place in range(16 * width):
            code, rest = divmod(place, width)
            index = 0
            for step, bit in enumerate(bits):
                index |= ((code >> (len(bits) - 1 - step)) & 1) << bit
            sources.append((index * pieces + piece) * width + rest)
    return np.array(sources, np.int32)


def picked(block, sources):
    rows = lax.broadcasted_iota(jnp.int32, (block.shape[-1], sources.shape[0]), 0)
    one_hot = (rows == sources[None, :]).astype(block.dtype)
    moved = jnp.einsum("blc,co->blo", block, one_hot, preferred_element_type=jnp.float32)
    return moved.astype(block.dtype)


CHAINS = (
    (("seq", 0), ("seq", 2), ("seq", 1), ("dp", 0), ("seq", 3), ("dp", 3), ("dp", 1), ("dp", 2)),
    (("seq", 0), ("seq", 1), ("dp", 0), ("seq", 2), ("seq", 3), ("dp", 3), ("dp", 1), ("dp", 2)),
    (("seq", 0), ("dp", 0), ("seq", 2), ("seq", 1), ("seq", 3), ("dp", 3), ("dp", 1), ("dp", 2)),
)


def gaussian_unit(value):
    return 0.5 * value * (1.0 + jax.scipy.special.erf(value * root_half))


def gaussian_slope(value):
    return 0.5 * (
        1.0 + jax.scipy.special.erf(value * root_half)
    ) + value * inv_root_two_pi * jnp.exp(-0.5 * value * value)


def windows(padded, length, taps):
    return jnp.stack([padded[:, offset : offset + length] for offset in range(taps)], axis=2)


def shards(features, weight, cotangent):
    taps = weight.shape[0]
    channels = weight.shape[2]
    batch = features.shape[0]
    length = features.shape[1]
    reach = taps // 2
    floats = features.astype(jnp.float32)
    inverse = lax.rsqrt(jnp.mean(floats * floats, axis=-1, keepdims=True) + epsilon)
    normed = floats * inverse
    activations = gaussian_unit(normed).astype(jnp.bfloat16)
    spread = (
        lax.broadcasted_iota(jnp.int32, (length, length // 2), 0) // 2
        == lax.broadcasted_iota(jnp.int32, (length, length // 2), 1)
    ).astype(cotangent.dtype)
    upward = 0.5 * jnp.einsum("bjc,lj->blc", cotangent, spread, preferred_element_type=jnp.float32)
    branch_grad = upward.astype(jnp.bfloat16)
    padded_acts = with_halo(activations, (("seq", 1),), reach)
    padded_grad = with_halo(branch_grad, (("seq", 1),), reach)
    dp_order = tuple(bit for axis, bit in CHAINS[0] if axis == "dp")
    act_window = windows(
        picked(padded_acts, jnp.asarray(sources_of(padded_acts.shape[-1], (dp_order,)))), length, taps
    )
    orders = [tuple(bit for axis, bit in steps if axis == "seq") for steps in CHAINS]
    columns = jnp.asarray(sources_of(channels, orders)).reshape(len(CHAINS), 2, -1)
    axis, bit = CHAINS[0][0]
    mine = (lax.axis_index(axis) >> bit) & 1
    halves = []
    for side in (mine, 1 - mine):
        chosen = lax.dynamic_index_in_dim(columns, side, axis=1, keepdims=False).reshape(-1)
        product = jnp.einsum(
            "blo,blki->oki", picked(branch_grad, chosen), act_window, preferred_element_type=jnp.float32
        )
        halves.append(product)
    partners = [(i, i ^ (1 << bit)) for i in range(lax.axis_size(axis))]
    partial = halves[0] + lax.ppermute(halves[1], axis, partners)
    partial = partial.reshape((len(CHAINS), -1) + partial.shape[1:])
    partial, padded_acts, padded_grad, floats, upward = lax.optimization_barrier(
        (partial, padded_acts, padded_grad, floats, upward)
    )
    inverse = lax.rsqrt(jnp.mean(floats * floats, axis=-1, keepdims=True) + epsilon)
    normed = floats * inverse
    grad_window = jnp.stack(
        [padded_grad[:, taps - 1 - k : taps - 1 - k + length] for k in range(taps)], axis=2
    )
    act_grad = jnp.einsum("blko,kio->bli", grad_window, weight, preferred_element_type=jnp.float32)
    slope_grad = act_grad * gaussian_slope(normed)
    centred = jnp.mean(slope_grad * floats, axis=-1, keepdims=True)
    input_grad = (upward + inverse * slope_grad - floats * inverse**3 * centred).astype(
        jnp.bfloat16
    )
    window = windows(padded_acts, length, taps)
    mixed = jnp.einsum("blki,kio->blo", window, weight, preferred_element_type=jnp.float32)
    summed = floats + mixed
    paired = summed.reshape(batch, length // 2, 2, channels)
    pooled = (0.5 * (paired[:, :, 0] + paired[:, :, 1])).astype(jnp.bfloat16)
    trunk_input = lax.all_to_all(pooled, "seq", split_axis=2, concat_axis=1, tiled=True)
    shared = [step for step in range(len(CHAINS[0])) if len({steps[step] for steps in CHAINS}) == 1]
    for step in range(1, len(CHAINS[0])):
        if step in shared:
            if isinstance(partial, list):
                partial = jnp.stack(partial)
            axis, bit = CHAINS[0][step]
            partial = halved(partial, axis, bit, 1 if axis == "seq" else 3)
            if step == shared[4]:
                partial, trunk_input = lax.optimization_barrier((partial, trunk_input))
        else:
            partial = [
                halved(partial[piece], axis, bit, 0 if axis == "seq" else 2)
                for piece, (axis, bit) in enumerate(steps[step] for steps in CHAINS)
            ]
    weight_grad = jnp.transpose(partial.reshape((-1,) + partial.shape[2:]), (1, 2, 0))
    return (trunk_input, input_grad, weight_grad)


def solution(mesh):
    return jax.shard_map(
        shards,
        mesh=mesh,
        in_specs=(P("dp", "seq", None), P(), P("dp", "seq", None)),
        out_specs=(P("dp", None, "seq"), P("dp", "seq", None), P(None, "dp", "seq")),
        check_vma=False,
    )
```
